256 devices in a mesh: dp: 8 (over z), seq: 32 (over x, y, core).
Axes of the slice: x: 4, y: 4, z: 8, core: 2. Of those that a mesh axis runs over, the one named last changes fastest.
Arguments:
- inputs: bfloat16 [8, 8192, 5120], P('dp', 'seq'), may hold values from -6 to 6
- gate_proj: bfloat16 [8, 8192, 5120], P('dp', 'seq'), may hold values from -6 to 6
- write_proj: bfloat16 [8, 8192, 128], P('dp', 'seq'), may hold values from -6 to 6
- read_proj: bfloat16 [8, 8192, 128], P('dp', 'seq'), may hold values from -6 to 6
- step_size: float32 [8, 80, 8192], P('dp', None, 'seq'), may hold values from 0 to 0.4, as said below
- log_forget: float32 [8, 80, 8192], P('dp', None, 'seq'), may hold values from -0.8 to 0, as said below
- conv_weight: float32 [4, 5376], replicated, may hold values from -3 to 3
- conv_bias: float32 [5376], replicated, may hold values from -3 to 3
- skip_gain: float32 [80], replicated, may hold values from 0.5 to 1.5
- norm_gain: float32 [5120], replicated, may hold values from 0.1 to 1.9
- code_weight: bfloat16 [5120, 256], P('dp'), may hold values from -0.5 to 0.5
- prior_draw: float32 [2048, 256], P(('dp', 'seq')), may hold values from -6 to 6
Outputs:
- mixed: bfloat16 [8, 8192, 5120], P('dp', 'seq')
- codes: float32 [2048, 256], P(('dp', 'seq'))
- kernel: float32 [2048, 4096], P(('dp', 'seq'))
The draws below stay inside these ranges and needn't reach their ends.
Inputs may be any that keep to these rules, and one draw needn't show every extreme that they name: `step_size`: positive step sizes, per document, head and position. `log_forget`: never positive.
All inputs are finite; a program needn't handle non-finite values.
Results may differ from the reference program's by a relative error of at most 0.008.
Values may be sent and summed in bfloat16 or wider, within the bound.
No kernel may reach another device: no remote copies, remote signals or barrier semaphores. Data moves between devices by JAX's collectives and lax.ppermute only.
A program may use at most 256 MiB of HBM per device.

```python
import math
import jax
import jax.numpy as jnp
from jax import lax

HEADS = 80
HEAD_DIM = 64
STATE = 128
CONV = 4
SPAN = 128
ZD = 256
SEG = 32
L_DEV = 256
CORPUS_SIZE = 8
TOKEN_SPAN = 8192
DI = 5120
CODES = 2048


def decay_plan(key):
    base = jax.random.fold_in(key, 7)
    slow_share = 0.5
    medium_share = 0.8
    pick = jax.random.uniform(jax.random.fold_in(base, 1), (HEADS,), jnp.float32)
    slow_rate = 0.4 / TOKEN_SPAN * jnp.exp(jax.random.uniform(jax.random.fold_in(base, 2), (HEADS,), jnp.float32, -0.693, 0.693))
    fast_rate = jnp.exp(jax.random.uniform(jax.random.fold_in(base, 3), (HEADS,), jnp.float32, jnp.log(1.0 / 50.0), jnp.log(1.0 / 20.0)))
    medium_rate = jnp.exp(jax.random.uniform(jax.random.fold_in(base, 4), (HEADS,), jnp.float32, jnp.log(1.5 / L_DEV), jnp.log(3.5 / L_DEV)))
    medium_rate = jnp.minimum(medium_rate, 0.05)
    return jnp.where(pick < slow_share, slow_rate, jnp.where(pick < medium_share, medium_rate, fast_rate))


def draw_log_forget(key, part):
    forgetting_factors = decay_plan(key)
    device_entries = jax.random.fold_in(key, 31)
    rough_approximation = jnp.exp(jax.random.uniform(jax.random.fold_in(device_entries, 1), (CORPUS_SIZE, HEADS, TOKEN_SPAN), jnp.float32, -0.693, 0.693))
    chosen_flare = jax.random.uniform(jax.random.fold_in(device_entries, 2), (CORPUS_SIZE, 1, TOKEN_SPAN), jnp.float32)
    recursion_levels = jax.random.uniform(jax.random.fold_in(device_entries, 3), (CORPUS_SIZE, 1, TOKEN_SPAN), jnp.float32, 0.22, 0.7)
    flare_clusters = jnp.where(chosen_flare < 3.0 / TOKEN_SPAN, recursion_levels, 0.0)
    return -(forgetting_factors[None, :, None] * rough_approximation) - flare_clusters


def draw_step_size(key, part):
    forgetting_factors = decay_plan(key)
    device_entries = jax.random.fold_in(key, 41)
    base = jnp.exp(jax.random.uniform(device_entries, (CORPUS_SIZE, HEADS, TOKEN_SPAN), jnp.float32, jnp.log(0.05), jnp.log(0.2)))
    return base * jnp.minimum(40.0 * forgetting_factors, 2.0)[None, :, None]


def shared_channels(key, channel_seed, width):
    factor_count = 6
    amplitude = 1.0
    noise_part = jax.random.normal(jax.random.fold_in(key, channel_seed + 1), (CORPUS_SIZE, TOKEN_SPAN, width), jnp.float32)
    factors = jax.random.normal(jax.random.fold_in(key, 101), (CORPUS_SIZE, TOKEN_SPAN, factor_count), jnp.float32)
    loadings = jax.random.normal(jax.random.fold_in(key, channel_seed), (CORPUS_SIZE, factor_count, width), jnp.float32)
    weight_each = amplitude / math.sqrt(factor_count)
    result = noise_part
    for factor_index in range(factor_count):
        result = result + weight_each * factors[:, :, factor_index:factor_index + 1] * loadings[:, factor_index:factor_index + 1, :]
    return jnp.clip(result, -6.0, 6.0).astype(jnp.bfloat16)


def draw_inputs(key, part):
    return shared_channels(key, 211, DI)


def draw_write_proj(key, part):
    return shared_channels(key, 307, STATE)


def shard_levels(own_key, shape, split, least, top_value):
    def one(axis_at, shards_of):
        heights = jax.random.uniform(jax.random.fold_in(jax.random.fold_in(own_key, 6), axis_at), (shards_of,), jnp.float32, least / len(split), top_value / len(split))
        return jnp.repeat(jnp.exp(heights), shape[axis_at] // shards_of).reshape((-1,) + (1,) * (len(shape) - axis_at - 1))

    factor_of = one(*split[0])
    for cut in split[1:]:
        factor_of = factor_of * one(*cut)
    return factor_of


def noise(stream_key, extent, scale, bound, cuts=(), kind=jnp.bfloat16):
    drawn = scale * jax.random.normal(stream_key, extent, jnp.float32)
    if cuts:
        drawn = drawn * shard_levels(stream_key, extent, cuts, -0.22, 0.18)
    return jnp.clip(drawn, -bound, bound).astype(kind)


def setup_inputs(seed: int = 0) -> dict:
    arg_keys = jax.random.split(jax.random.key(seed), 13)
    inputs = draw_inputs(jax.random.fold_in(arg_keys[12], 71), 0)
    gate_proj = noise(arg_keys[1], (CORPUS_SIZE, TOKEN_SPAN, DI), 1.0, 6.0, ((0, 8), (1, 32)))
    write_proj = draw_write_proj(jax.random.fold_in(arg_keys[12], 71), 0)
    read_proj = noise(arg_keys[3], (CORPUS_SIZE, TOKEN_SPAN, STATE), 1.0, 6.0, ((0, 8), (1, 32)))
    step_size = draw_step_size(jax.random.fold_in(arg_keys[12], 71), 0)
    log_forget = draw_log_forget(jax.random.fold_in(arg_keys[12], 71), 0)
    conv_weight = noise(arg_keys[6], (CONV, DI + 2 * STATE), CONV ** -0.5, 3.0, (), jnp.float32)
    conv_bias = noise(arg_keys[7], (DI + 2 * STATE,), 0.5, 3.0, (), jnp.float32)
    skip_gain = jnp.clip(jax.random.uniform(arg_keys[8], (HEADS,), jnp.float32, 0.5, 1.5), 0.5, 1.5)
    norm_gain = jnp.clip(1.0 + 0.18 * jax.random.normal(arg_keys[9], (DI,), jnp.float32), 0.1, 1.9)
    code_weight = noise(arg_keys[10], (DI, ZD), (DI // SEG) ** -0.5, 0.5, ((0, 8),))
    prior_draw = noise(arg_keys[11], (CODES, ZD), 1.0, 6.0, ((0, 256),), jnp.float32)
    return dict(inputs=inputs, gate_proj=gate_proj, write_proj=write_proj, read_proj=read_proj, step_size=step_size, log_forget=log_forget, conv_weight=conv_weight, conv_bias=conv_bias, skip_gain=skip_gain, norm_gain=norm_gain, code_weight=code_weight, prior_draw=prior_draw)


def block_terms(values, write_f, read_f, steps, logs):
    cum_log = jnp.cumsum(logs, axis=1)
    length = logs.shape[1]
    causal = jnp.arange(length)[:, None] >= jnp.arange(length)[None, :]
    scores = jnp.dot(read_f, write_f.T, precision=lax.Precision.HIGHEST)
    gap = jnp.where(causal[None], cum_log[:, :, None] - cum_log[:, None, :], 0.0)
    mixing = jnp.where(causal[None], scores[None] * jnp.exp(gap) * steps[:, None, :], 0.0)
    mixing = lax.optimization_barrier(mixing.astype(jnp.bfloat16)).astype(jnp.float32)
    inner_out = jnp.einsum('hts,shp->thp', mixing, values, precision=lax.Precision.HIGHEST)
    tail_decay = jnp.exp(cum_log[:, -1:] - cum_log) * steps
    weighted = tail_decay[:, :, None] * write_f[None]
    weighted = lax.optimization_barrier(weighted.astype(jnp.bfloat16)).astype(jnp.float32)
    states = jnp.einsum('hsn,shp->hpn', weighted, values, precision=lax.Precision.HIGHEST)
    return (inner_out, states, cum_log)

def document(pieces, conv_weight, conv_bias, skip_gain, norm_gain):
    inputs_doc, gate_doc, write_doc, read_doc, steps_doc, logs_doc = pieces
    blocks = TOKEN_SPAN // SPAN
    joined = jnp.concatenate([inputs_doc, write_doc, read_doc], axis=1).astype(jnp.float32)
    padded = jnp.pad(joined, ((CONV - 1, 0), (0, 0)))
    summed = conv_bias[None, :] + jnp.zeros_like(joined)
    for offset in range(CONV):
        summed = summed + conv_weight[offset][None, :] * padded[offset:offset + TOKEN_SPAN]
    active = jax.nn.silu(summed).astype(jnp.bfloat16).astype(jnp.float32)
    values = active[:, :DI].reshape(blocks, SPAN, HEADS, HEAD_DIM)
    write_f = active[:, DI:DI + STATE].reshape(blocks, SPAN, STATE)
    read_f = active[:, DI + STATE:].reshape(blocks, SPAN, STATE)
    steps = steps_doc.reshape(HEADS, blocks, SPAN).transpose(1, 0, 2)
    logs = logs_doc.reshape(HEADS, blocks, SPAN).transpose(1, 0, 2)

    def advance(carry, block_pieces):
        values_b, write_b, read_b, steps_b, logs_b = block_pieces
        inner_out, states, cum_log = block_terms(values_b, write_b, read_b, steps_b, logs_b)
        outer_out = jnp.exp(cum_log).T[:, :, None] * jnp.einsum('tn,hpn->thp', read_b, carry, precision=lax.Precision.HIGHEST)
        carry_next = jnp.exp(cum_log[:, -1])[:, None, None] * carry + states
        return (carry_next, inner_out + outer_out)
    start = jnp.zeros((HEADS, HEAD_DIM, STATE), jnp.float32)
    final_state, ssd_out = lax.scan(advance, start, (values, write_f, read_f, steps, logs))
    ssd_out = ssd_out.reshape(TOKEN_SPAN, HEADS, HEAD_DIM)
    total = ssd_out + skip_gain[None, :, None] * values.reshape(TOKEN_SPAN, HEADS, HEAD_DIM)
    gated = total.reshape(TOKEN_SPAN, DI) * jax.nn.silu(gate_doc.astype(jnp.float32))
    scale = lax.rsqrt(lax.optimization_barrier(jnp.mean(gated * gated, axis=1, keepdims=True)) + 1e-05)
    mixed_doc = (gated * scale * norm_gain[None, :]).astype(jnp.bfloat16)
    pooled = lax.optimization_barrier(jnp.mean(mixed_doc.astype(jnp.float32).reshape(TOKEN_SPAN // SEG, SEG, DI), axis=1)).astype(jnp.bfloat16)
    return (mixed_doc, pooled)

def reference(inputs, gate_proj, write_proj, read_proj, step_size, log_forget, conv_weight, conv_bias, skip_gain, norm_gain, code_weight, prior_draw):

    def one_doc(pieces):
        return document(pieces, conv_weight, conv_bias, skip_gain, norm_gain)
    mixed, pooled = lax.map(one_doc, (inputs, gate_proj, write_proj, read_proj, step_size, log_forget))
    codes = jnp.dot(pooled.reshape(CODES, DI), code_weight, preferred_element_type=jnp.float32)
    columns = jnp.concatenate([codes, prior_draw], axis=0)
    cross = jnp.dot(codes, columns.T, precision=lax.Precision.HIGHEST)
    row_sq = lax.optimization_barrier(jnp.sum(codes * codes, axis=1))
    col_sq = lax.optimization_barrier(jnp.sum(columns * columns, axis=1))
    dist_sq = row_sq[:, None] + col_sq[None, :] - 2.0 * cross
    kernel = 2.0 * ZD / (2.0 * ZD + dist_sq)
    return (mixed, codes, kernel)
```

```python
import jax
import jax.numpy as jnp
from jax import lax
from jax.sharding import PartitionSpec as P

SPAN = 128
SEG = 32
CORES = 2
RING = 4
XFER = jnp.bfloat16


def passed_along(block, axis, distance):
    devices = range(lax.axis_size(axis))
    route = [(i - distance, i) for i in devices if i - distance in devices]
    return lax.ppermute(block, axis, route)


def block_terms(values, write_rows, read_rows, steps, logs):
    cum_log = jnp.cumsum(logs, axis=1)
    length = logs.shape[1]
    causal = jnp.arange(length)[:, None] >= jnp.arange(length)[None, :]
    scores = jnp.dot(read_rows, write_rows.T, preferred_element_type=jnp.float32)
    decay = jnp.exp(jnp.where(causal[None], cum_log[:, :, None] - cum_log[:, None, :], -jnp.inf))
    mixing = (scores[None] * decay * steps[:, None, :]).astype(jnp.bfloat16)
    inner_out = jnp.einsum("hts,shp->thp", mixing, values, preferred_element_type=jnp.float32)
    tail_decay = jnp.exp(cum_log[:, -1:] - cum_log) * steps
    weighted = (tail_decay[:, :, None] * write_rows.astype(jnp.float32)[None]).astype(jnp.bfloat16)
    states = jnp.einsum("hsn,shp->hpn", weighted, values, preferred_element_type=jnp.float32)
    return (inner_out, states, cum_log)


def chip_routes(seq):
    rows = seq // (CORES * RING)

    def at(x, y, c):
        return (x * RING + y) * CORES + c

    cells = [(x, y) for x in range(rows) for y in range(RING)]
    up = [(at(x, y, 0), at(x, y, 1)) for x, y in cells]
    down = [(b, a) for a, b in up]
    y_fwd = [(at(x, y, 1), at(x, (y + 1) % RING, 1)) for x, y in cells]
    y_bwd = [(at(x, y, 1), at(x, (y - 1) % RING, 1)) for x, y in cells]
    x_fwd = [(at(x, y, 1), at((x + 1) % rows, y, 1)) for x, y in cells]
    x_bwd = [(at(x, y, 1), at((x - 1) % rows, y, 1)) for x, y in cells]
    return rows, up, down, (y_fwd, y_bwd), (x_fwd, x_bwd)


def ring_of_four(state, logsum, fwd, bwd):
    half = state.shape[0] // 2
    sent = state.astype(XFER)
    prev_state, prev_log = lax.ppermute((sent, logsum), "seq", fwd)
    next_state, next_log = lax.ppermute((sent, logsum), "seq", bwd)
    far_a, far_log = lax.ppermute((next_state[:half], next_log), "seq", bwd)
    far_b = lax.ppermute(prev_state[half:], "seq", fwd)
    far_state = jnp.concatenate([far_a, far_b], axis=0)
    return [
        (state, logsum, 0),
        (prev_state, prev_log, RING - 1),
        (next_state, next_log, 1),
        (far_state, far_log, 2),
    ]


def fold_ring(slots, pos):
    places = [(pos + k) % RING for (_, _, k) in slots]
    logs = [l for (_, l, _) in slots]
    zero = jnp.zeros_like(logs[0])
    before = None
    total = None
    for i, (value, _, _) in enumerate(slots):
        between = zero
        after = zero
        for j in range(len(slots)):
            if j == i:
                continue
            inside = (places[i] < places[j]) & (places[j] < pos)
            between = between + jnp.where(inside, logs[j], 0.0)
            after = after + jnp.where(places[i] < places[j], logs[j], 0.0)
        w_before = jnp.where(places[i] < pos, jnp.exp(between), 0.0)[:, None, None]
        w_total = jnp.exp(after)[:, None, None]
        v = value.astype(jnp.float32)
        before = w_before * v if before is None else before + w_before * v
        total = w_total * v if total is None else total + w_total * v
    lead = zero
    for j in range(len(slots)):
        lead = lead + jnp.where(places[j] < pos, logs[j], 0.0)
    total_log = sum(logs[1:], logs[0])
    return before, jnp.exp(lead), total, total_log


def carried_in(own_state, own_log):
    seq = lax.axis_size("seq")
    rows, up, down, y_routes, x_routes = chip_routes(seq)
    assert rows == RING and seq == rows * RING * CORES
    place = lax.axis_index("seq")
    core = place % CORES
    y_pos = (place // CORES) % RING
    x_pos = place // (CORES * RING)
    low_state, low_log = lax.ppermute((own_state, own_log), "seq", up)
    chip_state = jnp.exp(own_log)[:, None, None] * low_state + own_state
    chip_log = low_log + own_log
    slots = ring_of_four(chip_state, chip_log, *y_routes)
    row_before, row_lead, row_total, row_log = fold_ring(slots, y_pos)
    slots = ring_of_four(row_total, row_log, *x_routes)
    rows_before, _, _, _ = fold_ring(slots, x_pos)
    chip_in = row_lead[:, None, None] * rows_before + row_before
    chip_in_low = lax.ppermute(chip_in, "seq", down)
    high_in = jnp.exp(low_log)[:, None, None] * chip_in + low_state
    return jnp.where(core == 0, chip_in_low, high_in)


def gathered_rows(block):
    return lax.all_gather(lax.all_gather(block, "seq", axis=0, tiled=True), "dp", axis=0, tiled=True)


def per_device(
    inputs,
    gate_proj,
    write_proj,
    read_proj,
    step_size,
    log_forget,
    conv_weight,
    conv_bias,
    skip_gain,
    norm_gain,
    code_weight,
    prior_draw,
):
    length = inputs.shape[1]
    width = inputs.shape[2]
    state_dim = write_proj.shape[2]
    heads = step_size.shape[1]
    head_dim = width // heads
    taps = conv_weight.shape[0]
    all_prior = gathered_rows(prior_draw)
    full_code_weight = lax.all_gather(code_weight, "dp", axis=0, tiled=True)
    joined = jnp.concatenate([inputs[0], write_proj[0], read_proj[0]], axis=1)
    rim_rows = passed_along(joined[length - (taps - 1) :], "seq", 1)
    padded = jnp.concatenate([rim_rows, joined], axis=0)
    summed = conv_bias[None, :] + conv_weight[0][None, :] * padded[0:length].astype(jnp.float32)
    for offset in range(1, taps):
        summed = summed + conv_weight[offset][None, :] * padded[offset : offset + length].astype(
            jnp.float32
        )
    active = jax.nn.silu(summed).astype(jnp.bfloat16)
    values = active[:, :width].reshape(length, heads, head_dim)
    write_all = active[:, width : width + state_dim]
    read_all = active[:, width + state_dim :]
    steps = step_size[0]
    logs = log_forget[0]
    blocks = length // SPAN
    inner_list = []
    state_list = []
    cum_list = []
    for block in range(blocks):
        lower = block * SPAN
        upper = lower + SPAN
        inner_out, states, cum_log = block_terms(
            values[lower:upper],
            write_all[lower:upper],
            read_all[lower:upper],
            steps[:, lower:upper],
            logs[:, lower:upper],
        )
        inner_list.append(inner_out)
        state_list.append(states)
        cum_list.append(cum_log)
    running = jnp.zeros((heads, head_dim, state_dim), jnp.float32)
    before = jnp.zeros((heads,), jnp.float32)
    start_list = []
    before_list = []
    for block in range(blocks):
        start_list.append(running)
        before_list.append(before)
        block_total = cum_list[block][:, -1]
        running = jnp.exp(block_total)[:, None, None] * running + state_list[block]
        before = before + block_total
    carry_in = carried_in(running, before)
    outputs = []
    for block in range(blocks):
        lower = block * SPAN
        upper = lower + SPAN
        start = start_list[block] + jnp.exp(before_list[block])[:, None, None] * carry_in
        read_block = read_all[lower:upper].astype(jnp.float32)
        outer_out = jnp.exp(cum_list[block]).T[:, :, None] * jnp.einsum(
            "tn,hpn->thp", read_block, start, precision=lax.Precision.HIGHEST
        )
        outputs.append(inner_list[block] + outer_out)
    ssd_out = jnp.concatenate(outputs, axis=0)
    total = ssd_out + skip_gain[None, :, None] * values.astype(jnp.float32)
    gated = total.reshape(length, width) * jax.nn.silu(gate_proj[0].astype(jnp.float32))
    scale = lax.rsqrt(jnp.mean(gated * gated, axis=1, keepdims=True) + 1e-05)
    mixed = (gated * scale * norm_gain[None, :]).astype(jnp.bfloat16)
    pooled = jnp.mean(mixed.astype(jnp.float32).reshape(length // SEG, SEG, width), axis=1).astype(
        jnp.bfloat16
    )
    codes_local = jnp.dot(pooled, full_code_weight, preferred_element_type=jnp.float32)
    all_codes = gathered_rows(codes_local)
    columns = jnp.concatenate([all_codes, all_prior], axis=0)
    cross = jnp.dot(codes_local, columns.T, precision=lax.Precision.HIGHEST)
    row_sq = jnp.sum(codes_local * codes_local, axis=1)
    col_sq = jnp.sum(columns * columns, axis=1)
    dist_sq = row_sq[:, None] + col_sq[None, :] - 2.0 * cross
    code_dim = codes_local.shape[1]
    kernel = 2.0 * code_dim / (2.0 * code_dim + dist_sq)
    return (mixed[None], codes_local, kernel)


def solution(mesh):
    in_specs = (
        P("dp", "seq", None),
        P("dp", "seq", None),
        P("dp", "seq", None),
        P("dp", "seq", None),
        P("dp", None, "seq"),
        P("dp", None, "seq"),
        P(),
        P(),
        P(),
        P(),
        P("dp", None),
        P(("dp", "seq"), None),
    )
    out_specs = (P("dp", "seq", None), P(("dp", "seq"), None), P(("dp", "seq"), None))
    return jax.shard_map(
        per_device, mesh=mesh, in_specs=in_specs, out_specs=out_specs, check_vma=False
    )
```

```python
import jax
import jax.numpy as jnp
from jax import lax
from jax.sharding import PartitionSpec as P

SPAN = 128
SEG = 32
CORES = 2
RING = 4
XFER = jnp.bfloat16


def passed_along(block, axis, distance):
    devices = range(lax.axis_size(axis))
    route = [(i - distance, i) for i in devices if i - distance in devices]
    return lax.ppermute(block, axis, route)


def block_terms(values, write_rows, read_rows, steps, logs):
    cum_log = jnp.cumsum(logs, axis=1)
    length = logs.shape[1]
    causal = jnp.arange(length)[:, None] >= jnp.arange(length)[None, :]
    scores = jnp.dot(read_rows, write_rows.T, preferred_element_type=jnp.float32)
    decay = jnp.exp(jnp.where(causal[None], cum_log[:, :, None] - cum_log[:, None, :], -jnp.inf))
    mixing = (scores[None] * decay * steps[:, None, :]).astype(jnp.bfloat16)
    inner_out = jnp.einsum("hts,shp->thp", mixing, values, preferred_element_type=jnp.float32)
    tail_decay = jnp.exp(cum_log[:, -1:] - cum_log) * steps
    weighted = (tail_decay[:, :, None] * write_rows.astype(jnp.float32)[None]).astype(jnp.bfloat16)
    states = jnp.einsum("hsn,shp->hpn", weighted, values, preferred_element_type=jnp.float32)
    return (inner_out, states, cum_log)


def chip_routes(seq):
    rows = seq // (CORES * RING)

    def at(x, y, c):
        return (x * RING + y) * CORES + c

    cells = [(x, y) for x in range(rows) for y in range(RING)]
    up = [(at(x, y, 0), at(x, y, 1)) for x, y in cells]
    down = [(b, a) for a, b in up]
    y_fwd = [(at(x, y, 1), at(x, (y + 1) % RING, 1)) for x, y in cells]
    y_bwd = [(at(x, y, 1), at(x, (y - 1) % RING, 1)) for x, y in cells]
    x_fwd = [(at(x, y, 1), at((x + 1) % rows, y, 1)) for x, y in cells]
    x_bwd = [(at(x, y, 1), at((x - 1) % rows, y, 1)) for x, y in cells]
    return rows, up, down, (y_fwd, y_bwd), (x_fwd, x_bwd)


def ring_of_four(state, fwd, bwd):
    half = state.shape[0] // 2
    sent = state.astype(XFER)
    prev_state = lax.ppermute(sent, "seq", fwd)
    next_state = lax.ppermute(sent, "seq", bwd)
    far_a = lax.ppermute(next_state[:half], "seq", bwd)
    far_b = lax.ppermute(prev_state[half:], "seq", fwd)
    far_state = jnp.concatenate([far_a, far_b], axis=0)
    return [(state, 0), (prev_state, RING - 1), (next_state, 1), (far_state, 2)]


def fold_ring(slots, pos, ring_logs):
    places = [(pos + k) % RING for (_, k) in slots]
    logs = [lax.dynamic_index_in_dim(ring_logs, p, 0, False) for p in places]
    zero = jnp.zeros_like(logs[0])
    before = None
    total = None
    for i, (value, _) in enumerate(slots):
        between = zero
        after = zero
        for j in range(len(slots)):
            if j == i:
                continue
            inside = (places[i] < places[j]) & (places[j] < pos)
            between = between + jnp.where(inside, logs[j], 0.0)
            after = after + jnp.where(places[i] < places[j], logs[j], 0.0)
        w_before = jnp.where(places[i] < pos, jnp.exp(between), 0.0)[:, None, None]
        w_total = jnp.exp(after)[:, None, None]
        v = value.astype(jnp.float32)
        before = w_before * v if before is None else before + w_before * v
        total = w_total * v if total is None else total + w_total * v
    lead = zero
    for j in range(len(slots)):
        lead = lead + jnp.where(places[j] < pos, logs[j], 0.0)
    return before, jnp.exp(lead), total


def carried_in(own_state, shard_logs):
    seq = lax.axis_size("seq")
    rows, up, down, y_routes, x_routes = chip_routes(seq)
    assert rows == RING and seq == rows * RING * CORES
    place = lax.axis_index("seq")
    core = place % CORES
    y_pos = (place // CORES) % RING
    x_pos = place // (CORES * RING)
    grid_logs = shard_logs.reshape(rows, RING, CORES, -1)
    chip_logs = grid_logs[:, :, 0] + grid_logs[:, :, 1]
    own_log = lax.dynamic_index_in_dim(shard_logs, place, 0, False)
    low_log = lax.dynamic_index_in_dim(shard_logs, place - 1, 0, False)
    low_state = lax.ppermute(own_state, "seq", up)
    chip_state = jnp.exp(own_log)[:, None, None] * low_state + own_state
    slots = ring_of_four(chip_state, *y_routes)
    row_logs = lax.dynamic_index_in_dim(chip_logs, x_pos, 0, False)
    row_before, row_lead, row_total = fold_ring(slots, y_pos, row_logs)
    slots = ring_of_four(row_total, *x_routes)
    rows_before, _, _ = fold_ring(slots, x_pos, jnp.sum(chip_logs, axis=1))
    chip_in = row_lead[:, None, None] * rows_before + row_before
    chip_in_low = lax.ppermute(chip_in, "seq", down)
    high_in = jnp.exp(low_log)[:, None, None] * chip_in + low_state
    return jnp.where(core == 0, chip_in_low, high_in)


def placed(block, slots, index):
    held = jnp.zeros((slots,) + block.shape, block.dtype)
    return lax.dynamic_update_index_in_dim(held, block, index, 0)


def everywhere(block):
    flat = lax.axis_index("dp") * lax.axis_size("seq") + lax.axis_index("seq")
    count = lax.axis_size("dp") * lax.axis_size("seq")
    summed = lax.psum(placed(block, count, flat), ("dp", "seq"))
    return summed.reshape((count * block.shape[0],) + block.shape[1:])


def per_device(
    inputs,
    gate_proj,
    write_proj,
    read_proj,
    step_size,
    log_forget,
    conv_weight,
    conv_bias,
    skip_gain,
    norm_gain,
    code_weight,
    prior_draw,
):
    length = inputs.shape[1]
    width = inputs.shape[2]
    state_dim = write_proj.shape[2]
    heads = step_size.shape[1]
    head_dim = width // heads
    taps = conv_weight.shape[0]
    full_code_weight = lax.all_gather(code_weight, "dp", axis=0, tiled=True)
    joined = jnp.concatenate([inputs[0], write_proj[0], read_proj[0]], axis=1)
    rim_rows = passed_along(joined[length - (taps - 1) :], "seq", 1)
    padded = jnp.concatenate([rim_rows, joined], axis=0)
    summed = conv_bias[None, :] + conv_weight[0][None, :] * padded[0:length].astype(jnp.float32)
    for offset in range(1, taps):
        summed = summed + conv_weight[offset][None, :] * padded[offset : offset + length].astype(
            jnp.float32
        )
    active = jax.nn.silu(summed).astype(jnp.bfloat16)
    values = active[:, :width].reshape(length, heads, head_dim)
    write_all = active[:, width : width + state_dim]
    read_all = active[:, width + state_dim :]
    steps = step_size[0]
    logs = log_forget[0]
    blocks = length // SPAN
    inner_list = []
    state_list = []
    cum_list = []
    for block in range(blocks):
        lower = block * SPAN
        upper = lower + SPAN
        inner_out, states, cum_log = block_terms(
            values[lower:upper],
            write_all[lower:upper],
            read_all[lower:upper],
            steps[:, lower:upper],
            logs[:, lower:upper],
        )
        inner_list.append(inner_out)
        state_list.append(states)
        cum_list.append(cum_log)
    running = jnp.zeros((heads, head_dim, state_dim), jnp.float32)
    before = jnp.zeros((heads,), jnp.float32)
    start_list = []
    before_list = []
    for block in range(blocks):
        start_list.append(running)
        before_list.append(before)
        block_total = cum_list[block][:, -1]
        running = jnp.exp(block_total)[:, None, None] * running + state_list[block]
        before = before + block_total
    seq = lax.axis_size("seq")
    code_dim = prior_draw.shape[1]
    prior_size = prior_draw.shape[0] * code_dim
    shared = everywhere(jnp.concatenate([prior_draw.reshape(-1), before]))
    shared = shared.reshape(-1, prior_size + heads)
    all_prior = shared[:, :prior_size].reshape(-1, code_dim)
    shard_logs = lax.dynamic_slice_in_dim(shared[:, prior_size:], lax.axis_index("dp") * seq, seq, 0)
    carry_in = carried_in(running, shard_logs)
    outputs = []
    for block in range(blocks):
        lower = block * SPAN
        upper = lower + SPAN
        start = start_list[block] + jnp.exp(before_list[block])[:, None, None] * carry_in
        read_block = read_all[lower:upper].astype(jnp.float32)
        outer_out = jnp.exp(cum_list[block]).T[:, :, None] * jnp.einsum(
            "tn,hpn->thp", read_block, start, precision=lax.Precision.HIGHEST
        )
        outputs.append(inner_list[block] + outer_out)
    ssd_out = jnp.concatenate(outputs, axis=0)
    total = ssd_out + skip_gain[None, :, None] * values.astype(jnp.float32)
    gated = total.reshape(length, width) * jax.nn.silu(gate_proj[0].astype(jnp.float32))
    scale = lax.rsqrt(jnp.mean(gated * gated, axis=1, keepdims=True) + 1e-05)
    mixed = (gated * scale * norm_gain[None, :]).astype(jnp.bfloat16)
    pooled = jnp.mean(mixed.astype(jnp.float32).reshape(length // SEG, SEG, width), axis=1).astype(
        jnp.bfloat16
    )
    codes_local = jnp.dot(pooled, full_code_weight, preferred_element_type=jnp.float32)
    all_codes = everywhere(codes_local)
    columns = jnp.concatenate([all_codes, all_prior], axis=0)
    cross = jnp.dot(codes_local, columns.T, precision=lax.Precision.HIGHEST)
    row_sq = jnp.sum(codes_local * codes_local, axis=1)
    col_sq = jnp.sum(columns * columns, axis=1)
    dist_sq = row_sq[:, None] + col_sq[None, :] - 2.0 * cross
    kernel = 2.0 * code_dim / (2.0 * code_dim + dist_sq)
    return (mixed[None], codes_local, kernel)


def solution(mesh):
    in_specs = (
        P("dp", "seq", None),
        P("dp", "seq", None),
        P("dp", "seq", None),
        P("dp", "seq", None),
        P("dp", None, "seq"),
        P("dp", None, "seq"),
        P(),
        P(),
        P(),
        P(),
        P("dp", None),
        P(("dp", "seq"), None),
    )
    out_specs = (P("dp", "seq", None), P(("dp", "seq"), None), P(("dp", "seq"), None))
    return jax.shard_map(
        per_device, mesh=mesh, in_specs=in_specs, out_specs=out_specs, check_vma=False
    )
```

```python
import jax
import jax.numpy as jnp
from jax import lax
from jax.sharding import PartitionSpec as P

SPAN = 128
SEG = 32
CORES = 2
RING = 4
XFER = jnp.bfloat16


def passed_along(block, axis, distance):
    devices = range(lax.axis_size(axis))
    route = [(i - distance, i) for i in devices if i - distance in devices]
    return lax.ppermute(block, axis, route)


def block_terms(values, write_rows, read_rows, steps, logs):
    cum_log = jnp.cumsum(logs, axis=1)
    length = logs.shape[1]
    causal = jnp.arange(length)[:, None] >= jnp.arange(length)[None, :]
    scores = jnp.dot(read_rows, write_rows.T, preferred_element_type=jnp.float32)
    decay = jnp.exp(jnp.where(causal[None], cum_log[:, :, None] - cum_log[:, None, :], -jnp.inf))
    mixing = (scores[None] * decay * steps[:, None, :]).astype(jnp.bfloat16)
    inner_out = jnp.einsum("hts,shp->thp", mixing, values, preferred_element_type=jnp.float32)
    tail_decay = jnp.exp(cum_log[:, -1:] - cum_log) * steps
    weighted = (tail_decay[:, :, None] * write_rows.astype(jnp.float32)[None]).astype(jnp.bfloat16)
    states = jnp.einsum("hsn,shp->hpn", weighted, values, preferred_element_type=jnp.float32)
    return (inner_out, states, cum_log)


def chip_routes(seq):
    rows = seq // (CORES * RING)

    def at(x, y, c):
        return (x * RING + y) * CORES + c

    cells = [(x, y) for x in range(rows) for y in range(RING)]
    up = [(at(x, y, 0), at(x, y, 1)) for x, y in cells]
    down = [(b, a) for a, b in up]
    y_fwd = [(at(x, y, 1), at(x, (y + 1) % RING, 1)) for x, y in cells]
    y_bwd = [(at(x, y, 1), at(x, (y - 1) % RING, 1)) for x, y in cells]
    x_fwd = [(at(x, y, 1), at((x + 1) % rows, y, 1)) for x, y in cells]
    x_bwd = [(at(x, y, 1), at((x - 1) % rows, y, 1)) for x, y in cells]
    return rows, up, down, (y_fwd, y_bwd), (x_fwd, x_bwd)


def ring_of_four(state, fwd, bwd):
    half = state.shape[0] // 2
    sent = state.astype(XFER)
    prev_state = lax.ppermute(sent, "seq", fwd)
    next_state = lax.ppermute(sent, "seq", bwd)
    far_a = lax.ppermute(next_state[:half], "seq", bwd)
    far_b = lax.ppermute(prev_state[half:], "seq", fwd)
    far_state = jnp.concatenate([far_a, far_b], axis=0)
    return [(state, 0), (prev_state, RING - 1), (next_state, 1), (far_state, 2)]


def fold_ring(slots, pos, ring_logs):
    places = [(pos + k) % RING for (_, k) in slots]
    logs = [lax.dynamic_index_in_dim(ring_logs, p, 0, False) for p in places]
    zero = jnp.zeros_like(logs[0])
    before = None
    total = None
    for i, (value, _) in enumerate(slots):
        between = zero
        after = zero
        for j in range(len(slots)):
            if j == i:
                continue
            inside = (places[i] < places[j]) & (places[j] < pos)
            between = between + jnp.where(inside, logs[j], 0.0)
            after = after + jnp.where(places[i] < places[j], logs[j], 0.0)
        w_before = jnp.where(places[i] < pos, jnp.exp(between), 0.0)[:, None, None]
        w_total = jnp.exp(after)[:, None, None]
        v = value.astype(jnp.float32)
        before = w_before * v if before is None else before + w_before * v
        total = w_total * v if total is None else total + w_total * v
    lead = zero
    for j in range(len(slots)):
        lead = lead + jnp.where(places[j] < pos, logs[j], 0.0)
    return before, jnp.exp(lead), total


def carried_in(own_state, shard_logs):
    seq = lax.axis_size("seq")
    rows, up, down, y_routes, x_routes = chip_routes(seq)
    assert rows == RING and seq == rows * RING * CORES
    place = lax.axis_index("seq")
    core = place % CORES
    y_pos = (place // CORES) % RING
    x_pos = place // (CORES * RING)
    grid_logs = shard_logs.reshape(rows, RING, CORES, -1)
    chip_logs = grid_logs[:, :, 0] + grid_logs[:, :, 1]
    own_log = lax.dynamic_index_in_dim(shard_logs, place, 0, False)
    low_log = lax.dynamic_index_in_dim(shard_logs, place - 1, 0, False)
    low_state = lax.ppermute(own_state, "seq", up)
    chip_state = jnp.exp(own_log)[:, None, None] * low_state + own_state
    slots = ring_of_four(chip_state, *y_routes)
    row_logs = lax.dynamic_index_in_dim(chip_logs, x_pos, 0, False)
    row_before, row_lead, row_total = fold_ring(slots, y_pos, row_logs)
    slots = ring_of_four(row_total, *x_routes)
    rows_before, _, _ = fold_ring(slots, x_pos, jnp.sum(chip_logs, axis=1))
    chip_in = row_lead[:, None, None] * rows_before + row_before
    chip_in_low = lax.ppermute(chip_in, "seq", down)
    high_in = jnp.exp(low_log)[:, None, None] * chip_in + low_state
    return jnp.where(core == 0, chip_in_low, high_in)


def placed(block, slots, index):
    held = jnp.zeros((slots,) + block.shape, block.dtype)
    return lax.dynamic_update_index_in_dim(held, block, index, 0)


def everywhere(block):
    count = lax.axis_size("dp") * lax.axis_size("seq")
    spread = jnp.broadcast_to(block[None], (count,) + block.shape)
    got = lax.all_to_all(spread, ("dp", "seq"), 0, 0)
    return got.reshape((count * block.shape[0],) + block.shape[1:])


def per_device(
    inputs,
    gate_proj,
    write_proj,
    read_proj,
    step_size,
    log_forget,
    conv_weight,
    conv_bias,
    skip_gain,
    norm_gain,
    code_weight,
    prior_draw,
):
    length = inputs.shape[1]
    width = inputs.shape[2]
    state_dim = write_proj.shape[2]
    heads = step_size.shape[1]
    head_dim = width // heads
    taps = conv_weight.shape[0]
    full_code_weight = lax.all_gather(code_weight, "dp", axis=0, tiled=True)
    joined = jnp.concatenate([inputs[0], write_proj[0], read_proj[0]], axis=1)
    rim_rows = passed_along(joined[length - (taps - 1) :], "seq", 1)
    padded = jnp.concatenate([rim_rows, joined], axis=0)
    summed = conv_bias[None, :] + conv_weight[0][None, :] * padded[0:length].astype(jnp.float32)
    for offset in range(1, taps):
        summed = summed + conv_weight[offset][None, :] * padded[offset : offset + length].astype(
            jnp.float32
        )
    active = jax.nn.silu(summed).astype(jnp.bfloat16)
    values = active[:, :width].reshape(length, heads, head_dim)
    write_all = active[:, width : width + state_dim]
    read_all = active[:, width + state_dim :]
    steps = step_size[0]
    logs = log_forget[0]
    blocks = length // SPAN
    inner_list = []
    state_list = []
    cum_list = []
    for block in range(blocks):
        lower = block * SPAN
        upper = lower + SPAN
        inner_out, states, cum_log = block_terms(
            values[lower:upper],
            write_all[lower:upper],
            read_all[lower:upper],
            steps[:, lower:upper],
            logs[:, lower:upper],
        )
        inner_list.append(inner_out)
        state_list.append(states)
        cum_list.append(cum_log)
    running = jnp.zeros((heads, head_dim, state_dim), jnp.float32)
    before = jnp.zeros((heads,), jnp.float32)
    start_list = []
    before_list = []
    for block in range(blocks):
        start_list.append(running)
        before_list.append(before)
        block_total = cum_list[block][:, -1]
        running = jnp.exp(block_total)[:, None, None] * running + state_list[block]
        before = before + block_total
    seq = lax.axis_size("seq")
    code_dim = prior_draw.shape[1]
    prior_size = prior_draw.shape[0] * code_dim
    shared = everywhere(jnp.concatenate([prior_draw.reshape(-1), before]))
    shared = shared.reshape(-1, prior_size + heads)
    all_prior = shared[:, :prior_size].reshape(-1, code_dim)
    shard_logs = lax.dynamic_slice_in_dim(shared[:, prior_size:], lax.axis_index("dp") * seq, seq, 0)
    carry_in = carried_in(running, shard_logs)
    outputs = []
    for block in range(blocks):
        lower = block * SPAN
        upper = lower + SPAN
        start = start_list[block] + jnp.exp(before_list[block])[:, None, None] * carry_in
        read_block = read_all[lower:upper].astype(jnp.float32)
        outer_out = jnp.exp(cum_list[block]).T[:, :, None] * jnp.einsum(
            "tn,hpn->thp", read_block, start, precision=lax.Precision.HIGHEST
        )
        outputs.append(inner_list[block] + outer_out)
    ssd_out = jnp.concatenate(outputs, axis=0)
    total = ssd_out + skip_gain[None, :, None] * values.astype(jnp.float32)
    gated = total.reshape(length, width) * jax.nn.silu(gate_proj[0].astype(jnp.float32))
    scale = lax.rsqrt(jnp.mean(gated * gated, axis=1, keepdims=True) + 1e-05)
    mixed = (gated * scale * norm_gain[None, :]).astype(jnp.bfloat16)
    pooled = jnp.mean(mixed.astype(jnp.float32).reshape(length // SEG, SEG, width), axis=1).astype(
        jnp.bfloat16
    )
    codes_local = jnp.dot(pooled, full_code_weight, preferred_element_type=jnp.float32)
    all_codes = everywhere(codes_local)
    columns = jnp.concatenate([all_codes, all_prior], axis=0)
    cross = jnp.dot(codes_local, columns.T, precision=lax.Precision.HIGHEST)
    row_sq = jnp.sum(codes_local * codes_local, axis=1)
    col_sq = jnp.sum(columns * columns, axis=1)
    dist_sq = row_sq[:, None] + col_sq[None, :] - 2.0 * cross
    kernel = 2.0 * code_dim / (2.0 * code_dim + dist_sq)
    return (mixed[None], codes_local, kernel)


def solution(mesh):
    in_specs = (
        P("dp", "seq", None),
        P("dp", "seq", None),
        P("dp", "seq", None),
        P("dp", "seq", None),
        P("dp", None, "seq"),
        P("dp", None, "seq"),
        P(),
        P(),
        P(),
        P(),
        P("dp", None),
        P(("dp", "seq"), None),
    )
    out_specs = (P("dp", "seq", None), P(("dp", "seq"), None), P(("dp", "seq"), None))
    return jax.shard_map(
        per_device, mesh=mesh, in_specs=in_specs, out_specs=out_specs, check_vma=False
    )
```

```python
import jax
import jax.numpy as jnp
from jax import lax
from jax.sharding import PartitionSpec as P

SPAN = 128
SEG = 32
CORES = 2
RING = 4
XFER = jnp.bfloat16


def passed_along(block, axis, distance):
    devices = range(lax.axis_size(axis))
    route = [(i - distance, i) for i in devices if i - distance in devices]
    return lax.ppermute(block, axis, route)


def block_terms(values, write_rows, read_rows, steps, logs):
    cum_log = jnp.cumsum(logs, axis=1)
    length = logs.shape[1]
    causal = jnp.arange(length)[:, None] >= jnp.arange(length)[None, :]
    scores = jnp.dot(read_rows, write_rows.T, preferred_element_type=jnp.float32)
    decay = jnp.exp(jnp.where(causal[None], cum_log[:, :, None] - cum_log[:, None, :], -jnp.inf))
    mixing = (scores[None] * decay * steps[:, None, :]).astype(jnp.bfloat16)
    inner_out = jnp.einsum("hts,shp->thp", mixing, values, preferred_element_type=jnp.float32)
    tail_decay = jnp.exp(cum_log[:, -1:] - cum_log) * steps
    weighted = (tail_decay[:, :, None] * write_rows.astype(jnp.float32)[None]).astype(jnp.bfloat16)
    states = jnp.einsum("hsn,shp->hpn", weighted, values, preferred_element_type=jnp.float32)
    return (inner_out, states, cum_log)


def chip_routes(seq):
    rows = seq // (CORES * RING)

    def at(x, y, c):
        return (x * RING + y) * CORES + c

    cells = [(x, y) for x in range(rows) for y in range(RING)]
    up = [(at(x, y, 0), at(x, y, 1)) for x, y in cells]
    down = [(b, a) for a, b in up]
    y_fwd = [(at(x, y, 1), at(x, (y + 1) % RING, 1)) for x, y in cells]
    y_bwd = [(at(x, y, 1), at(x, (y - 1) % RING, 1)) for x, y in cells]
    x_fwd = [(at(x, y, 1), at((x + 1) % rows, y, 1)) for x, y in cells]
    x_bwd = [(at(x, y, 1), at((x - 1) % rows, y, 1)) for x, y in cells]
    return rows, up, down, (y_fwd, y_bwd), (x_fwd, x_bwd)


def ring_of_four(state, fwd, bwd):
    half = state.shape[0] // 2
    sent = state.astype(XFER)
    prev_state = lax.ppermute(sent, "seq", fwd)
    next_state = lax.ppermute(sent, "seq", bwd)
    far_a = lax.ppermute(next_state[:half], "seq", bwd)
    far_b = lax.ppermute(prev_state[half:], "seq", fwd)
    far_state = jnp.concatenate([far_a, far_b], axis=0)
    return [(state, 0), (prev_state, RING - 1), (next_state, 1), (far_state, 2)]


def fold_ring(slots, pos, ring_logs):
    places = [(pos + k) % RING for (_, k) in slots]
    logs = [lax.dynamic_index_in_dim(ring_logs, p, 0, False) for p in places]
    zero = jnp.zeros_like(logs[0])
    before = None
    total = None
    for i, (value, _) in enumerate(slots):
        between = zero
        after = zero
        for j in range(len(slots)):
            if j == i:
                continue
            inside = (places[i] < places[j]) & (places[j] < pos)
            between = between + jnp.where(inside, logs[j], 0.0)
            after = after + jnp.where(places[i] < places[j], logs[j], 0.0)
        w_before = jnp.where(places[i] < pos, jnp.exp(between), 0.0)[:, None, None]
        w_total = jnp.exp(after)[:, None, None]
        v = value.astype(jnp.float32)
        before = w_before * v if before is None else before + w_before * v
        total = w_total * v if total is None else total + w_total * v
    lead = zero
    for j in range(len(slots)):
        lead = lead + jnp.where(places[j] < pos, logs[j], 0.0)
    return before, jnp.exp(lead), total


def carried_in(own_state, shard_logs):
    seq = lax.axis_size("seq")
    rows, up, down, y_routes, x_routes = chip_routes(seq)
    assert rows == RING and seq == rows * RING * CORES
    place = lax.axis_index("seq")
    core = place % CORES
    y_pos = (place // CORES) % RING
    x_pos = place // (CORES * RING)
    grid_logs = shard_logs.reshape(rows, RING, CORES, -1)
    chip_logs = grid_logs[:, :, 0] + grid_logs[:, :, 1]
    own_log = lax.dynamic_index_in_dim(shard_logs, place, 0, False)
    low_log = lax.dynamic_index_in_dim(shard_logs, place - 1, 0, False)
    low_state = lax.ppermute(own_state, "seq", up)
    chip_state = jnp.exp(own_log)[:, None, None] * low_state + own_state
    slots = ring_of_four(chip_state, *y_routes)
    row_logs = lax.dynamic_index_in_dim(chip_logs, x_pos, 0, False)
    row_before, row_lead, row_total = fold_ring(slots, y_pos, row_logs)
    slots = ring_of_four(row_total, *x_routes)
    rows_before, _, _ = fold_ring(slots, x_pos, jnp.sum(chip_logs, axis=1))
    chip_in = row_lead[:, None, None] * rows_before + row_before
    chip_in_low = lax.ppermute(chip_in, "seq", down)
    high_in = jnp.exp(low_log)[:, None, None] * chip_in + low_state
    return jnp.where(core == 0, chip_in_low, high_in)


def placed(block, slots, index):
    held = jnp.zeros((slots,) + block.shape, block.dtype)
    return lax.dynamic_update_index_in_dim(held, block, index, 0)


def spread_over(block, axis):
    count = lax.axis_size(axis)
    return lax.all_to_all(jnp.broadcast_to(block[None], (count,) + block.shape), axis, 0, 0)


def prior_everywhere(block):
    rows = spread_over(block, "seq").reshape((-1,) + block.shape[1:])
    return lax.all_gather(rows, "dp", axis=0, tiled=True)


def codes_everywhere(block):
    rows = lax.all_gather(block, "dp", axis=0, tiled=False)
    got = spread_over(rows, "seq")
    return jnp.swapaxes(got, 0, 1).reshape((-1,) + block.shape[1:])


def per_device(
    inputs,
    gate_proj,
    write_proj,
    read_proj,
    step_size,
    log_forget,
    conv_weight,
    conv_bias,
    skip_gain,
    norm_gain,
    code_weight,
    prior_draw,
):
    length = inputs.shape[1]
    width = inputs.shape[2]
    state_dim = write_proj.shape[2]
    heads = step_size.shape[1]
    head_dim = width // heads
    taps = conv_weight.shape[0]
    full_code_weight = lax.all_gather(code_weight, "dp", axis=0, tiled=True)
    joined = jnp.concatenate([inputs[0], write_proj[0], read_proj[0]], axis=1)
    rim_rows = passed_along(joined[length - (taps - 1) :], "seq", 1)
    padded = jnp.concatenate([rim_rows, joined], axis=0)
    summed = conv_bias[None, :] + conv_weight[0][None, :] * padded[0:length].astype(jnp.float32)
    for offset in range(1, taps):
        summed = summed + conv_weight[offset][None, :] * padded[offset : offset + length].astype(
            jnp.float32
        )
    active = jax.nn.silu(summed).astype(jnp.bfloat16)
    values = active[:, :width].reshape(length, heads, head_dim)
    write_all = active[:, width : width + state_dim]
    read_all = active[:, width + state_dim :]
    steps = step_size[0]
    logs = log_forget[0]
    blocks = length // SPAN
    inner_list = []
    state_list = []
    cum_list = []
    for block in range(blocks):
        lower = block * SPAN
        upper = lower + SPAN
        inner_out, states, cum_log = block_terms(
            values[lower:upper],
            write_all[lower:upper],
            read_all[lower:upper],
            steps[:, lower:upper],
            logs[:, lower:upper],
        )
        inner_list.append(inner_out)
        state_list.append(states)
        cum_list.append(cum_log)
    running = jnp.zeros((heads, head_dim, state_dim), jnp.float32)
    before = jnp.zeros((heads,), jnp.float32)
    start_list = []
    before_list = []
    for block in range(blocks):
        start_list.append(running)
        before_list.append(before)
        block_total = cum_list[block][:, -1]
        running = jnp.exp(block_total)[:, None, None] * running + state_list[block]
        before = before + block_total
    all_prior = prior_everywhere(prior_draw)
    shard_logs = spread_over(before, "seq")
    carry_in = carried_in(running, shard_logs)
    all_prior, carry_in = lax.optimization_barrier((all_prior, carry_in))
    outputs = []
    for block in range(blocks):
        lower = block * SPAN
        upper = lower + SPAN
        start = start_list[block] + jnp.exp(before_list[block])[:, None, None] * carry_in
        read_block = read_all[lower:upper].astype(jnp.float32)
        outer_out = jnp.exp(cum_list[block]).T[:, :, None] * jnp.einsum(
            "tn,hpn->thp", read_block, start, precision=lax.Precision.HIGHEST
        )
        outputs.append(inner_list[block] + outer_out)
    ssd_out = jnp.concatenate(outputs, axis=0)
    total = ssd_out + skip_gain[None, :, None] * values.astype(jnp.float32)
    gated = total.reshape(length, width) * jax.nn.silu(gate_proj[0].astype(jnp.float32))
    scale = lax.rsqrt(jnp.mean(gated * gated, axis=1, keepdims=True) + 1e-05)
    mixed = (gated * scale * norm_gain[None, :]).astype(jnp.bfloat16)
    pooled = jnp.mean(mixed.astype(jnp.float32).reshape(length // SEG, SEG, width), axis=1).astype(
        jnp.bfloat16
    )
    codes_local = jnp.dot(pooled, full_code_weight, preferred_element_type=jnp.float32)
    all_codes = codes_everywhere(codes_local)
    columns = jnp.concatenate([all_codes, all_prior], axis=0)
    cross = jnp.dot(codes_local, columns.T, precision=lax.Precision.HIGHEST)
    row_sq = jnp.sum(codes_local * codes_local, axis=1)
    col_sq = jnp.sum(columns * columns, axis=1)
    dist_sq = row_sq[:, None] + col_sq[None, :] - 2.0 * cross
    code_dim = codes_local.shape[1]
    kernel = 2.0 * code_dim / (2.0 * code_dim + dist_sq)
    return (mixed[None], codes_local, kernel)


def solution(mesh):
    in_specs = (
        P("dp", "seq", None),
        P("dp", "seq", None),
        P("dp", "seq", None),
        P("dp", "seq", None),
        P("dp", None, "seq"),
        P("dp", None, "seq"),
        P(),
        P(),
        P(),
        P(),
        P("dp", None),
        P(("dp", "seq"), None),
    )
    out_specs = (P("dp", "seq", None), P(("dp", "seq"), None), P(("dp", "seq"), None))
    return jax.shard_map(
        per_device, mesh=mesh, in_specs=in_specs, out_specs=out_specs, check_vma=False
    )
```

```python
import jax
import jax.numpy as jnp
from jax import lax
from jax.sharding import PartitionSpec as P

SPAN = 128
SEG = 32
CORES = 2
RING = 4
XFER = jnp.bfloat16


def passed_along(block, axis, distance):
    devices = range(lax.axis_size(axis))
    route = [(i - distance, i) for i in devices if i - distance in devices]
    return lax.ppermute(block, axis, route)


def block_states(values, write_rows, steps, logs):
    cum_log = jnp.cumsum(logs, axis=1)
    tail_decay = jnp.exp(cum_log[:, -1:] - cum_log) * steps
    weighted = (tail_decay[:, :, None] * write_rows.astype(jnp.float32)[None]).astype(jnp.bfloat16)
    states = jnp.einsum("hsn,shp->hpn", weighted, values, preferred_element_type=jnp.float32)
    return (states, cum_log)


def block_inner(values, write_rows, read_rows, steps, cum_log):
    length = cum_log.shape[1]
    causal = jnp.arange(length)[:, None] >= jnp.arange(length)[None, :]
    scores = jnp.dot(read_rows, write_rows.T, preferred_element_type=jnp.float32)
    decay = jnp.exp(jnp.where(causal[None], cum_log[:, :, None] - cum_log[:, None, :], -jnp.inf))
    mixing = (scores[None] * decay * steps[:, None, :]).astype(jnp.bfloat16)
    return jnp.einsum("hts,shp->thp", mixing, values, preferred_element_type=jnp.float32)


def chip_routes(seq):
    rows = seq // (CORES * RING)

    def at(x, y, c):
        return (x * RING + y) * CORES + c

    cells = [(x, y) for x in range(rows) for y in range(RING)]
    up = [(at(x, y, 0), at(x, y, 1)) for x, y in cells]
    down = [(b, a) for a, b in up]
    y_fwd = [(at(x, y, 1), at(x, (y + 1) % RING, 1)) for x, y in cells]
    y_bwd = [(at(x, y, 1), at(x, (y - 1) % RING, 1)) for x, y in cells]
    x_fwd = [(at(x, y, 1), at((x + 1) % rows, y, 1)) for x, y in cells]
    x_bwd = [(at(x, y, 1), at((x - 1) % rows, y, 1)) for x, y in cells]
    return rows, up, down, (y_fwd, y_bwd), (x_fwd, x_bwd)


def exact_pieces(log):
    hi = lax.reduce_precision(log, exponent_bits=8, mantissa_bits=7)
    mid = lax.reduce_precision(log - hi, exponent_bits=8, mantissa_bits=7)
    return [hi, mid, log - hi - mid]


def packed(state, log):
    pieces = jnp.stack(exact_pieces(log), axis=-1)
    row = jnp.zeros((state.shape[0], 1, state.shape[2]), jnp.float32)
    row = row.at[:, 0, : pieces.shape[1]].set(pieces)
    return jnp.concatenate([state, row], axis=1).astype(XFER)


def unpacked(block):
    pieces = block[:, -1, :3].astype(jnp.float32)
    return block[:, :-1], (pieces[:, 0] + pieces[:, 1]) + pieces[:, 2]


def ring_of_four(state, log, fwd, bwd):
    half = state.shape[0] // 2
    sent = packed(state, log)
    prev_block = lax.ppermute(sent, "seq", fwd)
    next_block = lax.ppermute(sent, "seq", bwd)
    far_a = lax.ppermute(next_block[:half], "seq", bwd)
    far_b = lax.ppermute(prev_block[half:], "seq", fwd)
    far_block = jnp.concatenate([far_a, far_b], axis=0)
    slots = [(state, log, 0)]
    for block, k in ((prev_block, RING - 1), (next_block, 1), (far_block, 2)):
        value, value_log = unpacked(block)
        slots.append((value, value_log, k))
    return slots


def fold_ring(slots, pos):
    places = [(pos + k) % RING for (_, _, k) in slots]
    logs = [l for (_, l, _) in slots]
    zero = jnp.zeros_like(logs[0])
    before = None
    total = None
    for i, (value, _, _) in enumerate(slots):
        between = zero
        after = zero
        for j in range(len(slots)):
            if j == i:
                continue
            inside = (places[i] < places[j]) & (places[j] < pos)
            between = between + jnp.where(inside, logs[j], 0.0)
            after = after + jnp.where(places[i] < places[j], logs[j], 0.0)
        w_before = jnp.where(places[i] < pos, jnp.exp(between), 0.0)[:, None, None]
        w_total = jnp.exp(after)[:, None, None]
        v = value.astype(jnp.float32)
        before = w_before * v if before is None else before + w_before * v
        total = w_total * v if total is None else total + w_total * v
    lead = zero
    for j in range(len(slots)):
        lead = lead + jnp.where(places[j] < pos, logs[j], 0.0)
    return before, jnp.exp(lead), total, sum(logs[1:], logs[0])


def chip_ends(own_state, own_log):
    seq = lax.axis_size("seq")
    _, up, _, _, _ = chip_routes(seq)
    low_block = lax.ppermute(jnp.concatenate([own_state, jnp.broadcast_to(own_log[:, None, None], (own_state.shape[0], 1, own_state.shape[2]))], axis=1), "seq", up)
    return low_block[:, :-1], low_block[:, -1, 0]


def carried_in(own_state, own_log, low_state, low_log):
    seq = lax.axis_size("seq")
    rows, _, down, y_routes, x_routes = chip_routes(seq)
    assert rows == RING and seq == rows * RING * CORES
    place = lax.axis_index("seq")
    core = place % CORES
    y_pos = (place // CORES) % RING
    x_pos = place // (CORES * RING)
    chip_state = jnp.exp(own_log)[:, None, None] * low_state + own_state
    slots = ring_of_four(chip_state, low_log + own_log, *y_routes)
    row_before, row_lead, row_total, row_log = fold_ring(slots, y_pos)
    slots = ring_of_four(row_total, row_log, *x_routes)
    rows_before, _, _, _ = fold_ring(slots, x_pos)
    chip_in = row_lead[:, None, None] * rows_before + row_before
    chip_in_low = lax.ppermute(chip_in, "seq", down)
    high_in = jnp.exp(low_log)[:, None, None] * chip_in + low_state
    return jnp.where(core == 0, chip_in_low, high_in)


def placed(block, slots, index):
    held = jnp.zeros((slots,) + block.shape, block.dtype)
    return lax.dynamic_update_index_in_dim(held, block, index, 0)


def spread_over(block, axis):
    count = lax.axis_size(axis)
    return lax.all_to_all(jnp.broadcast_to(block[None], (count,) + block.shape), axis, 0, 0)


def prior_everywhere(block):
    rows = spread_over(block, "seq").reshape((-1,) + block.shape[1:])
    return lax.all_gather(rows, "dp", axis=0, tiled=True)


def codes_everywhere(block):
    rows = lax.all_gather(block, "dp", axis=0, tiled=False)
    got = spread_over(rows, "seq")
    return jnp.swapaxes(got, 0, 1).reshape((-1,) + block.shape[1:])


def per_device(
    inputs,
    gate_proj,
    write_proj,
    read_proj,
    step_size,
    log_forget,
    conv_weight,
    conv_bias,
    skip_gain,
    norm_gain,
    code_weight,
    prior_draw,
):
    length = inputs.shape[1]
    width = inputs.shape[2]
    state_dim = write_proj.shape[2]
    heads = step_size.shape[1]
    head_dim = width // heads
    taps = conv_weight.shape[0]
    full_code_weight = lax.all_gather(code_weight, "dp", axis=0, tiled=True)
    joined = jnp.concatenate([inputs[0], write_proj[0], read_proj[0]], axis=1)
    rim_rows = passed_along(joined[length - (taps - 1) :], "seq", 1)
    padded = jnp.concatenate([rim_rows, joined], axis=0)
    summed = conv_bias[None, :] + conv_weight[0][None, :] * padded[0:length].astype(jnp.float32)
    for offset in range(1, taps):
        summed = summed + conv_weight[offset][None, :] * padded[offset : offset + length].astype(
            jnp.float32
        )
    active = jax.nn.silu(summed).astype(jnp.bfloat16)
    values = active[:, :width].reshape(length, heads, head_dim)
    write_all = active[:, width : width + state_dim]
    read_all = active[:, width + state_dim :]
    steps = step_size[0]
    logs = log_forget[0]
    blocks = length // SPAN
    state_list = []
    cum_list = []
    for block in range(blocks):
        lower = block * SPAN
        upper = lower + SPAN
        states, cum_log = block_states(
            values[lower:upper], write_all[lower:upper], steps[:, lower:upper], logs[:, lower:upper]
        )
        state_list.append(states)
        cum_list.append(cum_log)
    running = jnp.zeros((heads, head_dim, state_dim), jnp.float32)
    before = jnp.zeros((heads,), jnp.float32)
    start_list = []
    before_list = []
    for block in range(blocks):
        start_list.append(running)
        before_list.append(before)
        block_total = cum_list[block][:, -1]
        running = jnp.exp(block_total)[:, None, None] * running + state_list[block]
        before = before + block_total
    all_prior = prior_everywhere(prior_draw)
    low_state, low_log = chip_ends(running, before)
    read_all, low_log = lax.optimization_barrier((read_all, low_log))
    inner_list = []
    for block in range(blocks):
        lower = block * SPAN
        upper = lower + SPAN
        inner_list.append(
            block_inner(
                values[lower:upper],
                write_all[lower:upper],
                read_all[lower:upper],
                steps[:, lower:upper],
                cum_list[block],
            )
        )
    carry_in = carried_in(running, before, low_state, low_log)
    all_prior, carry_in = lax.optimization_barrier((all_prior, carry_in))
    outputs = []
    for block in range(blocks):
        lower = block * SPAN
        upper = lower + SPAN
        start = start_list[block] + jnp.exp(before_list[block])[:, None, None] * carry_in
        read_block = read_all[lower:upper].astype(jnp.float32)
        outer_out = jnp.exp(cum_list[block]).T[:, :, None] * jnp.einsum(
            "tn,hpn->thp", read_block, start, precision=lax.Precision.HIGHEST
        )
        outputs.append(inner_list[block] + outer_out)
    ssd_out = jnp.concatenate(outputs, axis=0)
    total = ssd_out + skip_gain[None, :, None] * values.astype(jnp.float32)
    gated = total.reshape(length, width) * jax.nn.silu(gate_proj[0].astype(jnp.float32))
    scale = lax.rsqrt(jnp.mean(gated * gated, axis=1, keepdims=True) + 1e-05)
    mixed = (gated * scale * norm_gain[None, :]).astype(jnp.bfloat16)
    pooled = jnp.mean(mixed.astype(jnp.float32).reshape(length // SEG, SEG, width), axis=1).astype(
        jnp.bfloat16
    )
    codes_local = jnp.dot(pooled, full_code_weight, preferred_element_type=jnp.float32)
    all_codes = codes_everywhere(codes_local)
    columns = jnp.concatenate([all_codes, all_prior], axis=0)
    cross = jnp.dot(codes_local, columns.T, precision=lax.Precision.HIGHEST)
    row_sq = jnp.sum(codes_local * codes_local, axis=1)
    col_sq = jnp.sum(columns * columns, axis=1)
    dist_sq = row_sq[:, None] + col_sq[None, :] - 2.0 * cross
    code_dim = codes_local.shape[1]
    kernel = 2.0 * code_dim / (2.0 * code_dim + dist_sq)
    return (mixed[None], codes_local, kernel)


def solution(mesh):
    in_specs = (
        P("dp", "seq", None),
        P("dp", "seq", None),
        P("dp", "seq", None),
        P("dp", "seq", None),
        P("dp", None, "seq"),
        P("dp", None, "seq"),
        P(),
        P(),
        P(),
        P(),
        P("dp", None),
        P(("dp", "seq"), None),
    )
    out_specs = (P("dp", "seq", None), P(("dp", "seq"), None), P(("dp", "seq"), None))
    return jax.shard_map(
        per_device, mesh=mesh, in_specs=in_specs, out_specs=out_specs, check_vma=False
    )
```

```python
import jax
import jax.numpy as jnp
from jax import lax
from jax.sharding import PartitionSpec as P

SPAN = 128
SEG = 32
CORES = 2
RING = 4
XFER = jnp.bfloat16


def passed_along(block, axis, distance):
    devices = range(lax.axis_size(axis))
    route = [(i - distance, i) for i in devices if i - distance in devices]
    return lax.ppermute(block, axis, route)


def block_terms(values, write_rows, read_rows, steps, logs):
    cum_log = jnp.cumsum(logs, axis=1)
    length = logs.shape[1]
    causal = jnp.arange(length)[:, None] >= jnp.arange(length)[None, :]
    scores = jnp.dot(read_rows, write_rows.T, preferred_element_type=jnp.float32)
    decay = jnp.exp(jnp.where(causal[None], cum_log[:, :, None] - cum_log[:, None, :], -jnp.inf))
    mixing = (scores[None] * decay * steps[:, None, :]).astype(jnp.bfloat16)
    inner_out = jnp.einsum("hts,shp->thp", mixing, values, preferred_element_type=jnp.float32)
    tail_decay = jnp.exp(cum_log[:, -1:] - cum_log) * steps
    weighted = (tail_decay[:, :, None] * write_rows.astype(jnp.float32)[None]).astype(jnp.bfloat16)
    states = jnp.einsum("hsn,shp->hpn", weighted, values, preferred_element_type=jnp.float32)
    return (inner_out, states, cum_log)


def chip_routes(seq):
    rows = seq // (CORES * RING)

    def at(x, y, c):
        return (x * RING + y) * CORES + c

    cells = [(x, y) for x in range(rows) for y in range(RING)]
    up = [(at(x, y, 0), at(x, y, 1)) for x, y in cells]
    down = [(b, a) for a, b in up]
    y_fwd = [(at(x, y, 1), at(x, (y + 1) % RING, 1)) for x, y in cells]
    y_bwd = [(at(x, y, 1), at(x, (y - 1) % RING, 1)) for x, y in cells]
    x_fwd = [(at(x, y, 1), at((x + 1) % rows, y, 1)) for x, y in cells]
    x_bwd = [(at(x, y, 1), at((x - 1) % rows, y, 1)) for x, y in cells]
    return rows, up, down, (y_fwd, y_bwd), (x_fwd, x_bwd)


def ring_of_four(state, fwd, bwd):
    half = state.shape[0] // 2
    sent = state.astype(XFER)
    prev_state = lax.ppermute(sent, "seq", fwd)
    next_state = lax.ppermute(sent, "seq", bwd)
    far_a = lax.ppermute(next_state[:half], "seq", bwd)
    far_b = lax.ppermute(prev_state[half:], "seq", fwd)
    far_state = jnp.concatenate([far_a, far_b], axis=0)
    return [(state, 0), (prev_state, RING - 1), (next_state, 1), (far_state, 2)]


def fold_ring(slots, pos, ring_logs):
    places = [(pos + k) % RING for (_, k) in slots]
    logs = [lax.dynamic_index_in_dim(ring_logs, p, 0, False) for p in places]
    zero = jnp.zeros_like(logs[0])
    before = None
    total = None
    for i, (value, _) in enumerate(slots):
        between = zero
        after = zero
        for j in range(len(slots)):
            if j == i:
                continue
            inside = (places[i] < places[j]) & (places[j] < pos)
            between = between + jnp.where(inside, logs[j], 0.0)
            after = after + jnp.where(places[i] < places[j], logs[j], 0.0)
        w_before = jnp.where(places[i] < pos, jnp.exp(between), 0.0)[:, None, None]
        w_total = jnp.exp(after)[:, None, None]
        v = value.astype(jnp.float32)
        before = w_before * v if before is None else before + w_before * v
        total = w_total * v if total is None else total + w_total * v
    lead = zero
    for j in range(len(slots)):
        lead = lead + jnp.where(places[j] < pos, logs[j], 0.0)
    return before, jnp.exp(lead), total


def carried_in(own_state, shard_logs):
    seq = lax.axis_size("seq")
    rows, up, down, y_routes, x_routes = chip_routes(seq)
    assert rows == RING and seq == rows * RING * CORES
    place = lax.axis_index("seq")
    core = place % CORES
    y_pos = (place // CORES) % RING
    x_pos = place // (CORES * RING)
    grid_logs = shard_logs.reshape(rows, RING, CORES, -1)
    chip_logs = grid_logs[:, :, 0] + grid_logs[:, :, 1]
    own_log = lax.dynamic_index_in_dim(shard_logs, place, 0, False)
    low_log = lax.dynamic_index_in_dim(shard_logs, place - 1, 0, False)
    low_state = lax.ppermute(own_state, "seq", up)
    chip_state = jnp.exp(own_log)[:, None, None] * low_state + own_state
    slots = ring_of_four(chip_state, *y_routes)
    row_logs = lax.dynamic_index_in_dim(chip_logs, x_pos, 0, False)
    row_before, row_lead, row_total = fold_ring(slots, y_pos, row_logs)
    slots = ring_of_four(row_total, *x_routes)
    rows_before, _, _ = fold_ring(slots, x_pos, jnp.sum(chip_logs, axis=1))
    chip_in = row_lead[:, None, None] * rows_before + row_before
    chip_in_low = lax.ppermute(chip_in, "seq", down)
    high_in = jnp.exp(low_log)[:, None, None] * chip_in + low_state
    return jnp.where(core == 0, chip_in_low, high_in)


def placed(block, slots, index):
    held = jnp.zeros((slots,) + block.shape, block.dtype)
    return lax.dynamic_update_index_in_dim(held, block, index, 0)


def spread_over(block, axis):
    count = lax.axis_size(axis)
    return lax.all_to_all(jnp.broadcast_to(block[None], (count,) + block.shape), axis, 0, 0)


def prior_everywhere(block):
    rows = spread_over(block, "seq").reshape((-1,) + block.shape[1:])
    return lax.all_gather(rows, "dp", axis=0, tiled=True)


def codes_everywhere(block):
    rows = spread_over(block.astype(XFER), "dp")
    got = spread_over(rows, "seq")
    return jnp.swapaxes(got, 0, 1).reshape((-1,) + block.shape[1:]).astype(jnp.float32)


def per_device(
    inputs,
    gate_proj,
    write_proj,
    read_proj,
    step_size,
    log_forget,
    conv_weight,
    conv_bias,
    skip_gain,
    norm_gain,
    code_weight,
    prior_draw,
):
    length = inputs.shape[1]
    width = inputs.shape[2]
    state_dim = write_proj.shape[2]
    heads = step_size.shape[1]
    head_dim = width // heads
    taps = conv_weight.shape[0]
    full_code_weight = lax.all_gather(code_weight, "dp", axis=0, tiled=True)
    joined = jnp.concatenate([inputs[0], write_proj[0], read_proj[0]], axis=1)
    rim_rows = passed_along(joined[length - (taps - 1) :], "seq", 1)
    padded = jnp.concatenate([rim_rows, joined], axis=0)
    summed = conv_bias[None, :] + conv_weight[0][None, :] * padded[0:length].astype(jnp.float32)
    for offset in range(1, taps):
        summed = summed + conv_weight[offset][None, :] * padded[offset : offset + length].astype(
            jnp.float32
        )
    active = jax.nn.silu(summed).astype(jnp.bfloat16)
    values = active[:, :width].reshape(length, heads, head_dim)
    write_all = active[:, width : width + state_dim]
    read_all = active[:, width + state_dim :]
    steps = step_size[0]
    logs = log_forget[0]
    blocks = length // SPAN
    inner_list = []
    state_list = []
    cum_list = []
    for block in range(blocks):
        lower = block * SPAN
        upper = lower + SPAN
        inner_out, states, cum_log = block_terms(
            values[lower:upper],
            write_all[lower:upper],
            read_all[lower:upper],
            steps[:, lower:upper],
            logs[:, lower:upper],
        )
        inner_list.append(inner_out)
        state_list.append(states)
        cum_list.append(cum_log)
    running = jnp.zeros((heads, head_dim, state_dim), jnp.float32)
    before = jnp.zeros((heads,), jnp.float32)
    start_list = []
    before_list = []
    for block in range(blocks):
        start_list.append(running)
        before_list.append(before)
        block_total = cum_list[block][:, -1]
        running = jnp.exp(block_total)[:, None, None] * running + state_list[block]
        before = before + block_total
    all_prior = prior_everywhere(prior_draw)
    shard_logs = spread_over(before, "seq")
    carry_in = carried_in(running, shard_logs)
    all_prior, carry_in = lax.optimization_barrier((all_prior, carry_in))
    outputs = []
    for block in range(blocks):
        lower = block * SPAN
        upper = lower + SPAN
        start = start_list[block] + jnp.exp(before_list[block])[:, None, None] * carry_in
        read_block = read_all[lower:upper].astype(jnp.float32)
        outer_out = jnp.exp(cum_list[block]).T[:, :, None] * jnp.einsum(
            "tn,hpn->thp", read_block, start, precision=lax.Precision.HIGHEST
        )
        outputs.append(inner_list[block] + outer_out)
    ssd_out = jnp.concatenate(outputs, axis=0)
    total = ssd_out + skip_gain[None, :, None] * values.astype(jnp.float32)
    gated = total.reshape(length, width) * jax.nn.silu(gate_proj[0].astype(jnp.float32))
    scale = lax.rsqrt(jnp.mean(gated * gated, axis=1, keepdims=True) + 1e-05)
    mixed = (gated * scale * norm_gain[None, :]).astype(jnp.bfloat16)
    pooled = jnp.mean(mixed.astype(jnp.float32).reshape(length // SEG, SEG, width), axis=1).astype(
        jnp.bfloat16
    )
    codes_local = jnp.dot(pooled, full_code_weight, preferred_element_type=jnp.float32)
    all_codes = codes_everywhere(codes_local)
    columns = jnp.concatenate([all_codes, all_prior], axis=0)
    cross = jnp.dot(codes_local, columns.T, precision=lax.Precision.HIGHEST)
    row_sq = jnp.sum(codes_local * codes_local, axis=1)
    col_sq = jnp.sum(columns * columns, axis=1)
    dist_sq = row_sq[:, None] + col_sq[None, :] - 2.0 * cross
    code_dim = codes_local.shape[1]
    kernel = 2.0 * code_dim / (2.0 * code_dim + dist_sq)
    return (mixed[None], codes_local, kernel)


def solution(mesh):
    in_specs = (
        P("dp", "seq", None),
        P("dp", "seq", None),
        P("dp", "seq", None),
        P("dp", "seq", None),
        P("dp", None, "seq"),
        P("dp", None, "seq"),
        P(),
        P(),
        P(),
        P(),
        P("dp", None),
        P(("dp", "seq"), None),
    )
    out_specs = (P("dp", "seq", None), P(("dp", "seq"), None), P(("dp", "seq"), None))
    return jax.shard_map(
        per_device, mesh=mesh, in_specs=in_specs, out_specs=out_specs, check_vma=False
    )
```

```python
import jax
import jax.numpy as jnp
from jax import lax
from jax.sharding import PartitionSpec as P

SPAN = 128
SEG = 32
CORES = 2
RING = 4
XFER = jnp.bfloat16


def passed_along(block, axis, distance):
    devices = range(lax.axis_size(axis))
    route = [(i - distance, i) for i in devices if i - distance in devices]
    return lax.ppermute(block, axis, route)


def block_terms(values, write_rows, read_rows, steps, logs):
    cum_log = jnp.cumsum(logs, axis=1)
    length = logs.shape[1]
    causal = jnp.arange(length)[:, None] >= jnp.arange(length)[None, :]
    scores = jnp.dot(read_rows, write_rows.T, preferred_element_type=jnp.float32)
    decay = jnp.exp(jnp.where(causal[None], cum_log[:, :, None] - cum_log[:, None, :], -jnp.inf))
    mixing = (scores[None] * decay * steps[:, None, :]).astype(jnp.bfloat16)
    inner_out = jnp.einsum("hts,shp->thp", mixing, values, preferred_element_type=jnp.float32)
    tail_decay = jnp.exp(cum_log[:, -1:] - cum_log) * steps
    weighted = (tail_decay[:, :, None] * write_rows.astype(jnp.float32)[None]).astype(jnp.bfloat16)
    states = jnp.einsum("hsn,shp->hpn", weighted, values, preferred_element_type=jnp.float32)
    return (inner_out, states, cum_log)


def chip_routes(seq):
    rows = seq // (CORES * RING)

    def at(x, y, c):
        return (x * RING + y) * CORES + c

    cells = [(x, y) for x in range(rows) for y in range(RING)]
    up = [(at(x, y, 0), at(x, y, 1)) for x, y in cells]
    down = [(b, a) for a, b in up]
    y_fwd = [(at(x, y, 1), at(x, (y + 1) % RING, 1)) for x, y in cells]
    y_bwd = [(at(x, y, 1), at(x, (y - 1) % RING, 1)) for x, y in cells]
    x_fwd = [(at(x, y, 1), at((x + 1) % rows, y, 1)) for x, y in cells]
    x_bwd = [(at(x, y, 1), at((x - 1) % rows, y, 1)) for x, y in cells]
    return rows, up, down, (y_fwd, y_bwd), (x_fwd, x_bwd)


def exact_pieces(log):
    hi = lax.reduce_precision(log, exponent_bits=8, mantissa_bits=7)
    mid = lax.reduce_precision(log - hi, exponent_bits=8, mantissa_bits=7)
    return [hi, mid, log - hi - mid]


def packed(state, log):
    pieces = jnp.stack(exact_pieces(log), axis=-1)
    row = jnp.zeros((state.shape[0], 1, state.shape[2]), jnp.float32)
    row = row.at[:, 0, : pieces.shape[1]].set(pieces)
    return jnp.concatenate([state, row], axis=1).astype(XFER)


def unpacked(block):
    pieces = block[:, -1, :3].astype(jnp.float32)
    return block[:, :-1], (pieces[:, 0] + pieces[:, 1]) + pieces[:, 2]


def ring_of_four(state, log, fwd, bwd):
    half = state.shape[0] // 2
    sent = packed(state, log)
    prev_block = lax.ppermute(sent, "seq", fwd)
    next_block = lax.ppermute(sent, "seq", bwd)
    far_a = lax.ppermute(next_block[:half], "seq", bwd)
    far_b = lax.ppermute(prev_block[half:], "seq", fwd)
    far_block = jnp.concatenate([far_a, far_b], axis=0)
    slots = [(state, log, 0)]
    for block, k in ((prev_block, RING - 1), (next_block, 1), (far_block, 2)):
        value, value_log = unpacked(block)
        slots.append((value, value_log, k))
    return slots


def fold_ring(slots, pos):
    places = [(pos + k) % RING for (_, _, k) in slots]
    logs = [l for (_, l, _) in slots]
    zero = jnp.zeros_like(logs[0])
    before = None
    total = None
    for i, (value, _, _) in enumerate(slots):
        between = zero
        after = zero
        for j in range(len(slots)):
            if j == i:
                continue
            inside = (places[i] < places[j]) & (places[j] < pos)
            between = between + jnp.where(inside, logs[j], 0.0)
            after = after + jnp.where(places[i] < places[j], logs[j], 0.0)
        w_before = jnp.where(places[i] < pos, jnp.exp(between), 0.0)[:, None, None]
        w_total = jnp.exp(after)[:, None, None]
        v = value.astype(jnp.float32)
        before = w_before * v if before is None else before + w_before * v
        total = w_total * v if total is None else total + w_total * v
    lead = zero
    for j in range(len(slots)):
        lead = lead + jnp.where(places[j] < pos, logs[j], 0.0)
    return before, jnp.exp(lead), total, sum(logs[1:], logs[0])


def chip_ends(own_state, own_log):
    seq = lax.axis_size("seq")
    _, up, _, _, _ = chip_routes(seq)
    low_block = lax.ppermute(jnp.concatenate([own_state, jnp.broadcast_to(own_log[:, None, None], (own_state.shape[0], 1, own_state.shape[2]))], axis=1), "seq", up)
    return low_block[:, :-1], low_block[:, -1, 0]


def carried_in(own_state, own_log, low_state, low_log):
    seq = lax.axis_size("seq")
    rows, _, down, y_routes, x_routes = chip_routes(seq)
    assert rows == RING and seq == rows * RING * CORES
    place = lax.axis_index("seq")
    core = place % CORES
    y_pos = (place // CORES) % RING
    x_pos = place // (CORES * RING)
    chip_state = jnp.exp(own_log)[:, None, None] * low_state + own_state
    slots = ring_of_four(chip_state, low_log + own_log, *y_routes)
    row_before, row_lead, row_total, row_log = fold_ring(slots, y_pos)
    slots = ring_of_four(row_total, row_log, *x_routes)
    rows_before, _, _, _ = fold_ring(slots, x_pos)
    chip_in = row_lead[:, None, None] * rows_before + row_before
    chip_in_low = lax.ppermute(chip_in, "seq", down)
    high_in = jnp.exp(low_log)[:, None, None] * chip_in + low_state
    return jnp.where(core == 0, chip_in_low, high_in)


def placed(block, slots, index):
    held = jnp.zeros((slots,) + block.shape, block.dtype)
    return lax.dynamic_update_index_in_dim(held, block, index, 0)


def spread_over(block, axis):
    count = lax.axis_size(axis)
    return lax.all_to_all(jnp.broadcast_to(block[None], (count,) + block.shape), axis, 0, 0)


def prior_everywhere(block):
    rows = spread_over(block, "seq").reshape((-1,) + block.shape[1:])
    return lax.all_gather(rows, "dp", axis=0, tiled=True)


def codes_everywhere(block):
    rows = spread_over(block.astype(XFER), "dp")
    got = spread_over(rows, "seq")
    return jnp.swapaxes(got, 0, 1).reshape((-1,) + block.shape[1:]).astype(jnp.float32)


def per_device(
    inputs,
    gate_proj,
    write_proj,
    read_proj,
    step_size,
    log_forget,
    conv_weight,
    conv_bias,
    skip_gain,
    norm_gain,
    code_weight,
    prior_draw,
):
    length = inputs.shape[1]
    width = inputs.shape[2]
    state_dim = write_proj.shape[2]
    heads = step_size.shape[1]
    head_dim = width // heads
    taps = conv_weight.shape[0]
    full_code_weight = lax.all_gather(code_weight, "dp", axis=0, tiled=True)
    joined = jnp.concatenate([inputs[0], write_proj[0], read_proj[0]], axis=1)
    rim_rows = passed_along(joined[length - (taps - 1) :], "seq", 1)
    padded = jnp.concatenate([rim_rows, joined], axis=0)
    summed = conv_bias[None, :] + conv_weight[0][None, :] * padded[0:length].astype(jnp.float32)
    for offset in range(1, taps):
        summed = summed + conv_weight[offset][None, :] * padded[offset : offset + length].astype(
            jnp.float32
        )
    active = jax.nn.silu(summed).astype(jnp.bfloat16)
    values = active[:, :width].reshape(length, heads, head_dim)
    write_all = active[:, width : width + state_dim]
    read_all = active[:, width + state_dim :]
    steps = step_size[0]
    logs = log_forget[0]
    blocks = length // SPAN
    inner_list = []
    state_list = []
    cum_list = []
    for block in range(blocks):
        lower = block * SPAN
        upper = lower + SPAN
        inner_out, states, cum_log = block_terms(
            values[lower:upper],
            write_all[lower:upper],
            read_all[lower:upper],
            steps[:, lower:upper],
            logs[:, lower:upper],
        )
        inner_list.append(inner_out)
        state_list.append(states)
        cum_list.append(cum_log)
    running = jnp.zeros((heads, head_dim, state_dim), jnp.float32)
    before = jnp.zeros((heads,), jnp.float32)
    start_list = []
    before_list = []
    for block in range(blocks):
        start_list.append(running)
        before_list.append(before)
        block_total = cum_list[block][:, -1]
        running = jnp.exp(block_total)[:, None, None] * running + state_list[block]
        before = before + block_total
    all_prior = prior_everywhere(prior_draw)
    low_state, low_log = chip_ends(running, before)
    carry_in = carried_in(running, before, low_state, low_log)
    all_prior, carry_in = lax.optimization_barrier((all_prior, carry_in))
    outputs = []
    for block in range(blocks):
        lower = block * SPAN
        upper = lower + SPAN
        start = start_list[block] + jnp.exp(before_list[block])[:, None, None] * carry_in
        read_block = read_all[lower:upper].astype(jnp.float32)
        outer_out = jnp.exp(cum_list[block]).T[:, :, None] * jnp.einsum(
            "tn,hpn->thp", read_block, start, precision=lax.Precision.HIGHEST
        )
        outputs.append(inner_list[block] + outer_out)
    ssd_out = jnp.concatenate(outputs, axis=0)
    total = ssd_out + skip_gain[None, :, None] * values.astype(jnp.float32)
    gated = total.reshape(length, width) * jax.nn.silu(gate_proj[0].astype(jnp.float32))
    scale = lax.rsqrt(jnp.mean(gated * gated, axis=1, keepdims=True) + 1e-05)
    mixed = (gated * scale * norm_gain[None, :]).astype(jnp.bfloat16)
    pooled = jnp.mean(mixed.astype(jnp.float32).reshape(length // SEG, SEG, width), axis=1).astype(
        jnp.bfloat16
    )
    codes_local = jnp.dot(pooled, full_code_weight, preferred_element_type=jnp.float32)
    all_codes = codes_everywhere(codes_local)
    columns = jnp.concatenate([all_codes, all_prior], axis=0)
    cross = jnp.dot(codes_local, columns.T, precision=lax.Precision.HIGHEST)
    row_sq = jnp.sum(codes_local * codes_local, axis=1)
    col_sq = jnp.sum(columns * columns, axis=1)
    dist_sq = row_sq[:, None] + col_sq[None, :] - 2.0 * cross
    code_dim = codes_local.shape[1]
    kernel = 2.0 * code_dim / (2.0 * code_dim + dist_sq)
    return (mixed[None], codes_local, kernel)


def solution(mesh):
    in_specs = (
        P("dp", "seq", None),
        P("dp", "seq", None),
        P("dp", "seq", None),
        P("dp", "seq", None),
        P("dp", None, "seq"),
        P("dp", None, "seq"),
        P(),
        P(),
        P(),
        P(),
        P("dp", None),
        P(("dp", "seq"), None),
    )
    out_specs = (P("dp", "seq", None), P(("dp", "seq"), None), P(("dp", "seq"), None))
    return jax.shard_map(
        per_device, mesh=mesh, in_specs=in_specs, out_specs=out_specs, check_vma=False
    )
```

```python
import jax
import jax.numpy as jnp
from jax import lax
from jax.sharding import PartitionSpec as P

SPAN = 128
SEG = 32
CORES = 2
RING = 4
XFER = jnp.bfloat16


def passed_along(block, axis, distance):
    devices = range(lax.axis_size(axis))
    route = [(i - distance, i) for i in devices if i - distance in devices]
    return lax.ppermute(block, axis, route)


def block_terms(values, write_rows, read_rows, steps, logs):
    cum_log = jnp.cumsum(logs, axis=1)
    length = logs.shape[1]
    causal = jnp.arange(length)[:, None] >= jnp.arange(length)[None, :]
    scores = jnp.dot(read_rows, write_rows.T, preferred_element_type=jnp.float32)
    decay = jnp.exp(jnp.where(causal[None], cum_log[:, :, None] - cum_log[:, None, :], -jnp.inf))
    mixing = (scores[None] * decay * steps[:, None, :]).astype(jnp.bfloat16)
    inner_out = jnp.einsum("hts,shp->thp", mixing, values, preferred_element_type=jnp.float32)
    tail_decay = jnp.exp(cum_log[:, -1:] - cum_log) * steps
    weighted = (tail_decay[:, :, None] * write_rows.astype(jnp.float32)[None]).astype(jnp.bfloat16)
    states = jnp.einsum("hsn,shp->hpn", weighted, values, preferred_element_type=jnp.float32)
    return (inner_out, states, cum_log)


def chip_routes(seq):
    rows = seq // (CORES * RING)

    def at(x, y, c):
        return (x * RING + y) * CORES + c

    cells = [(x, y, c) for x in range(rows) for y in range(RING) for c in range(CORES)]
    partner = [(at(x, y, c), at(x, y, 1 - c)) for x, y, c in cells]
    y_fwd = [(at(x, y, c), at(x, (y + 1) % RING, c)) for x, y, c in cells]
    y_bwd = [(at(x, y, c), at(x, (y - 1) % RING, c)) for x, y, c in cells]
    x_fwd = [(at(x, y, c), at((x + 1) % rows, y, c)) for x, y, c in cells]
    x_bwd = [(at(x, y, c), at((x - 1) % rows, y, c)) for x, y, c in cells]
    return rows, partner, (y_fwd, y_bwd), (x_fwd, x_bwd)


def ring_of_four(state, fwd, bwd):
    half = state.shape[0] // 2
    sent = state.astype(XFER)
    prev_state = lax.ppermute(sent, "seq", fwd)
    next_state = lax.ppermute(sent, "seq", bwd)
    far_a = lax.ppermute(next_state[:half], "seq", bwd)
    far_b = lax.ppermute(prev_state[half:], "seq", fwd)
    far_state = jnp.concatenate([far_a, far_b], axis=0)
    return [(state, 0), (prev_state, RING - 1), (next_state, 1), (far_state, 2)]


def fold_ring(slots, pos, ring_logs):
    places = [(pos + k) % RING for (_, k) in slots]
    logs = [lax.dynamic_index_in_dim(ring_logs, p, 0, False) for p in places]
    zero = jnp.zeros_like(logs[0])
    before = None
    total = None
    for i, (value, _) in enumerate(slots):
        between = zero
        after = zero
        for j in range(len(slots)):
            if j == i:
                continue
            inside = (places[i] < places[j]) & (places[j] < pos)
            between = between + jnp.where(inside, logs[j], 0.0)
            after = after + jnp.where(places[i] < places[j], logs[j], 0.0)
        w_before = jnp.where(places[i] < pos, jnp.exp(between), 0.0)[:, None, None]
        w_total = jnp.exp(after)[:, None, None]
        v = value.astype(jnp.float32)
        before = w_before * v if before is None else before + w_before * v
        total = w_total * v if total is None else total + w_total * v
    lead = zero
    for j in range(len(slots)):
        lead = lead + jnp.where(places[j] < pos, logs[j], 0.0)
    return before, jnp.exp(lead), total


def carried_in(own_state, shard_logs):
    seq = lax.axis_size("seq")
    rows, partner, y_routes, x_routes = chip_routes(seq)
    assert rows == RING and seq == rows * RING * CORES
    place = lax.axis_index("seq")
    core = place % CORES
    y_pos = (place // CORES) % RING
    x_pos = place // (CORES * RING)
    half = own_state.shape[0] // CORES
    mine = core * half
    theirs = (1 - core) * half
    grid_logs = shard_logs.reshape(rows, RING, CORES, -1)
    chip_logs = lax.dynamic_slice_in_dim(grid_logs[:, :, 0] + grid_logs[:, :, 1], mine, half, 2)
    low_log = lax.dynamic_slice_in_dim(grid_logs[x_pos, y_pos, 0], mine, half, 0)
    high_log = lax.dynamic_slice_in_dim(grid_logs[x_pos, y_pos, 1], mine, half, 0)
    own_half = lax.dynamic_slice_in_dim(own_state, mine, half, 0)
    other_half = lax.ppermute(lax.dynamic_slice_in_dim(own_state, theirs, half, 0), "seq", partner)
    low_half = jnp.where(core == 0, own_half, other_half)
    high_half = jnp.where(core == 0, other_half, own_half)
    chip_state = jnp.exp(high_log)[:, None, None] * low_half + high_half
    slots = ring_of_four(chip_state, *y_routes)
    row_logs = lax.dynamic_index_in_dim(chip_logs, x_pos, 0, False)
    row_before, row_lead, row_total = fold_ring(slots, y_pos, row_logs)
    slots = ring_of_four(row_total, *x_routes)
    rows_before, _, _ = fold_ring(slots, x_pos, jnp.sum(chip_logs, axis=1))
    chip_in = row_lead[:, None, None] * rows_before + row_before
    high_in = jnp.exp(low_log)[:, None, None] * chip_in + low_half
    keep = jnp.where(core == 0, chip_in, high_in)
    give = jnp.where(core == 0, high_in, chip_in)
    got = lax.ppermute(give, "seq", partner)
    return jnp.where(core == 0, jnp.concatenate([keep, got], 0), jnp.concatenate([got, keep], 0))


def placed(block, slots, index):
    held = jnp.zeros((slots,) + block.shape, block.dtype)
    return lax.dynamic_update_index_in_dim(held, block, index, 0)


def spread_over(block, axis):
    count = lax.axis_size(axis)
    return lax.all_to_all(jnp.broadcast_to(block[None], (count,) + block.shape), axis, 0, 0)


def prior_everywhere(block):
    rows = spread_over(block, "seq").reshape((-1,) + block.shape[1:])
    return lax.all_gather(rows, "dp", axis=0, tiled=True)


def codes_everywhere(block):
    rows = spread_over(block.astype(XFER), "dp")
    got = spread_over(rows, "seq")
    return jnp.swapaxes(got, 0, 1).reshape((-1,) + block.shape[1:]).astype(jnp.float32)


def per_device(
    inputs,
    gate_proj,
    write_proj,
    read_proj,
    step_size,
    log_forget,
    conv_weight,
    conv_bias,
    skip_gain,
    norm_gain,
    code_weight,
    prior_draw,
):
    length = inputs.shape[1]
    width = inputs.shape[2]
    state_dim = write_proj.shape[2]
    heads = step_size.shape[1]
    head_dim = width // heads
    taps = conv_weight.shape[0]
    full_code_weight = lax.all_gather(code_weight, "dp", axis=0, tiled=True)
    joined = jnp.concatenate([inputs[0], write_proj[0], read_proj[0]], axis=1)
    rim_rows = passed_along(joined[length - (taps - 1) :], "seq", 1)
    padded = jnp.concatenate([rim_rows, joined], axis=0)
    summed = conv_bias[None, :] + conv_weight[0][None, :] * padded[0:length].astype(jnp.float32)
    for offset in range(1, taps):
        summed = summed + conv_weight[offset][None, :] * padded[offset : offset + length].astype(
            jnp.float32
        )
    active = jax.nn.silu(summed).astype(jnp.bfloat16)
    values = active[:, :width].reshape(length, heads, head_dim)
    write_all = active[:, width : width + state_dim]
    read_all = active[:, width + state_dim :]
    steps = step_size[0]
    logs = log_forget[0]
    blocks = length // SPAN
    inner_list = []
    state_list = []
    cum_list = []
    for block in range(blocks):
        lower = block * SPAN
        upper = lower + SPAN
        inner_out, states, cum_log = block_terms(
            values[lower:upper],
            write_all[lower:upper],
            read_all[lower:upper],
            steps[:, lower:upper],
            logs[:, lower:upper],
        )
        inner_list.append(inner_out)
        state_list.append(states)
        cum_list.append(cum_log)
    running = jnp.zeros((heads, head_dim, state_dim), jnp.float32)
    before = jnp.zeros((heads,), jnp.float32)
    start_list = []
    before_list = []
    for block in range(blocks):
        start_list.append(running)
        before_list.append(before)
        block_total = cum_list[block][:, -1]
        running = jnp.exp(block_total)[:, None, None] * running + state_list[block]
        before = before + block_total
    all_prior = prior_everywhere(prior_draw)
    shard_logs = spread_over(before, "seq")
    carry_in = carried_in(running, shard_logs)
    all_prior, carry_in = lax.optimization_barrier((all_prior, carry_in))
    outputs = []
    for block in range(blocks):
        lower = block * SPAN
        upper = lower + SPAN
        start = start_list[block] + jnp.exp(before_list[block])[:, None, None] * carry_in
        read_block = read_all[lower:upper].astype(jnp.float32)
        outer_out = jnp.exp(cum_list[block]).T[:, :, None] * jnp.einsum(
            "tn,hpn->thp", read_block, start, precision=lax.Precision.HIGHEST
        )
        outputs.append(inner_list[block] + outer_out)
    ssd_out = jnp.concatenate(outputs, axis=0)
    total = ssd_out + skip_gain[None, :, None] * values.astype(jnp.float32)
    gated = total.reshape(length, width) * jax.nn.silu(gate_proj[0].astype(jnp.float32))
    scale = lax.rsqrt(jnp.mean(gated * gated, axis=1, keepdims=True) + 1e-05)
    mixed = (gated * scale * norm_gain[None, :]).astype(jnp.bfloat16)
    pooled = jnp.mean(mixed.astype(jnp.float32).reshape(length // SEG, SEG, width), axis=1).astype(
        jnp.bfloat16
    )
    codes_local = jnp.dot(pooled, full_code_weight, preferred_element_type=jnp.float32)
    all_codes = codes_everywhere(codes_local)
    columns = jnp.concatenate([all_codes, all_prior], axis=0)
    cross = jnp.dot(codes_local, columns.T, precision=lax.Precision.HIGHEST)
    row_sq = jnp.sum(codes_local * codes_local, axis=1)
    col_sq = jnp.sum(columns * columns, axis=1)
    dist_sq = row_sq[:, None] + col_sq[None, :] - 2.0 * cross
    code_dim = codes_local.shape[1]
    kernel = 2.0 * code_dim / (2.0 * code_dim + dist_sq)
    return (mixed[None], codes_local, kernel)


def solution(mesh):
    in_specs = (
        P("dp", "seq", None),
        P("dp", "seq", None),
        P("dp", "seq", None),
        P("dp", "seq", None),
        P("dp", None, "seq"),
        P("dp", None, "seq"),
        P(),
        P(),
        P(),
        P(),
        P("dp", None),
        P(("dp", "seq"), None),
    )
    out_specs = (P("dp", "seq", None), P(("dp", "seq"), None), P(("dp", "seq"), None))
    return jax.shard_map(
        per_device, mesh=mesh, in_specs=in_specs, out_specs=out_specs, check_vma=False
    )
```

```python
import jax
import jax.numpy as jnp
from jax import lax
from jax.sharding import PartitionSpec as P

SPAN = 128
SEG = 32
CORES = 2
RING = 4
XFER = jnp.bfloat16


def passed_along(block, axis, distance):
    devices = range(lax.axis_size(axis))
    route = [(i - distance, i) for i in devices if i - distance in devices]
    return lax.ppermute(block, axis, route)


def block_terms(values, write_rows, read_rows, steps, logs):
    cum_log = jnp.cumsum(logs, axis=1)
    length = logs.shape[1]
    causal = jnp.arange(length)[:, None] >= jnp.arange(length)[None, :]
    scores = jnp.dot(read_rows, write_rows.T, preferred_element_type=jnp.float32)
    decay = jnp.exp(jnp.where(causal[None], cum_log[:, :, None] - cum_log[:, None, :], -jnp.inf))
    mixing = (scores[None] * decay * steps[:, None, :]).astype(jnp.bfloat16)
    inner_out = jnp.einsum("hts,shp->thp", mixing, values, preferred_element_type=jnp.float32)
    tail_decay = jnp.exp(cum_log[:, -1:] - cum_log) * steps
    weighted = (tail_decay[:, :, None] * write_rows.astype(jnp.float32)[None]).astype(jnp.bfloat16)
    states = jnp.einsum("hsn,shp->hpn", weighted, values, preferred_element_type=jnp.float32)
    return (inner_out, states, cum_log)


def chip_routes(seq):
    rows = seq // (CORES * RING)

    def at(x, y, c):
        return (x * RING + y) * CORES + c

    cells = [(x, y, c) for x in range(rows) for y in range(RING) for c in range(CORES)]
    partner = [(at(x, y, c), at(x, y, 1 - c)) for x, y, c in cells]
    y_fwd = [(at(x, y, c), at(x, (y + 1) % RING, c)) for x, y, c in cells]
    y_bwd = [(at(x, y, c), at(x, (y - 1) % RING, c)) for x, y, c in cells]
    x_fwd = [(at(x, y, c), at((x + 1) % rows, y, c)) for x, y, c in cells]
    x_bwd = [(at(x, y, c), at((x - 1) % rows, y, c)) for x, y, c in cells]
    return rows, partner, (y_fwd, y_bwd), (x_fwd, x_bwd)


def ring_of_four(state, fwd, bwd):
    half = state.shape[0] // 2
    sent = state.astype(XFER)
    prev_state = lax.ppermute(sent, "seq", fwd)
    next_state = lax.ppermute(sent, "seq", bwd)
    far_a = lax.ppermute(next_state[:half], "seq", bwd)
    far_b = lax.ppermute(prev_state[half:], "seq", fwd)
    far_state = jnp.concatenate([far_a, far_b], axis=0)
    return [(state, 0), (prev_state, RING - 1), (next_state, 1), (far_state, 2)]


def fold_ring(slots, pos, ring_logs):
    places = [(pos + k) % RING for (_, k) in slots]
    logs = [lax.dynamic_index_in_dim(ring_logs, p, 0, False) for p in places]
    zero = jnp.zeros_like(logs[0])
    before = None
    total = None
    for i, (value, _) in enumerate(slots):
        between = zero
        after = zero
        for j in range(len(slots)):
            if j == i:
                continue
            inside = (places[i] < places[j]) & (places[j] < pos)
            between = between + jnp.where(inside, logs[j], 0.0)
            after = after + jnp.where(places[i] < places[j], logs[j], 0.0)
        w_before = jnp.where(places[i] < pos, jnp.exp(between), 0.0)[:, None, None]
        w_total = jnp.exp(after)[:, None, None]
        v = value.astype(jnp.float32)
        before = w_before * v if before is None else before + w_before * v
        total = w_total * v if total is None else total + w_total * v
    lead = zero
    for j in range(len(slots)):
        lead = lead + jnp.where(places[j] < pos, logs[j], 0.0)
    return before, jnp.exp(lead), total


def carried_in(own_state, shard_logs, prior_block):
    seq = lax.axis_size("seq")
    rows, partner, y_routes, x_routes = chip_routes(seq)
    assert rows == RING and seq == rows * RING * CORES
    place = lax.axis_index("seq")
    core = place % CORES
    y_pos = (place // CORES) % RING
    x_pos = place // (CORES * RING)
    half = own_state.shape[0] // CORES
    mine = core * half
    theirs = (1 - core) * half
    grid_logs = shard_logs.reshape(rows, RING, CORES, -1)
    chip_logs = lax.dynamic_slice_in_dim(grid_logs[:, :, 0] + grid_logs[:, :, 1], mine, half, 2)
    low_log = lax.dynamic_slice_in_dim(grid_logs[x_pos, y_pos, 0], mine, half, 0)
    high_log = lax.dynamic_slice_in_dim(grid_logs[x_pos, y_pos, 1], mine, half, 0)
    own_half = lax.dynamic_slice_in_dim(own_state, mine, half, 0)
    other_half = lax.ppermute(lax.dynamic_slice_in_dim(own_state, theirs, half, 0), "seq", partner)
    low_half = jnp.where(core == 0, own_half, other_half)
    high_half = jnp.where(core == 0, other_half, own_half)
    chip_state = jnp.exp(high_log)[:, None, None] * low_half + high_half
    slots = ring_of_four(chip_state, *y_routes)
    row_logs = lax.dynamic_index_in_dim(chip_logs, x_pos, 0, False)
    row_before, row_lead, row_total = fold_ring(slots, y_pos, row_logs)
    prior_block, row_total = lax.optimization_barrier((prior_block, row_total))
    all_prior = prior_everywhere(prior_block)
    slots = ring_of_four(row_total, *x_routes)
    rows_before, _, _ = fold_ring(slots, x_pos, jnp.sum(chip_logs, axis=1))
    chip_in = row_lead[:, None, None] * rows_before + row_before
    high_in = jnp.exp(low_log)[:, None, None] * chip_in + low_half
    keep = jnp.where(core == 0, chip_in, high_in)
    give = jnp.where(core == 0, high_in, chip_in)
    got = lax.ppermute(give, "seq", partner)
    carry = jnp.where(core == 0, jnp.concatenate([keep, got], 0), jnp.concatenate([got, keep], 0))
    return carry, all_prior


def placed(block, slots, index):
    held = jnp.zeros((slots,) + block.shape, block.dtype)
    return lax.dynamic_update_index_in_dim(held, block, index, 0)


def spread_over(block, axis):
    count = lax.axis_size(axis)
    return lax.all_to_all(jnp.broadcast_to(block[None], (count,) + block.shape), axis, 0, 0)


def prior_everywhere(block):
    rows = spread_over(block, "seq").reshape((-1,) + block.shape[1:])
    return lax.all_gather(rows, "dp", axis=0, tiled=True)


def codes_everywhere(block):
    rows = spread_over(block.astype(XFER), "dp")
    got = spread_over(rows, "seq")
    return jnp.swapaxes(got, 0, 1).reshape((-1,) + block.shape[1:]).astype(jnp.float32)


def per_device(
    inputs,
    gate_proj,
    write_proj,
    read_proj,
    step_size,
    log_forget,
    conv_weight,
    conv_bias,
    skip_gain,
    norm_gain,
    code_weight,
    prior_draw,
):
    length = inputs.shape[1]
    width = inputs.shape[2]
    state_dim = write_proj.shape[2]
    heads = step_size.shape[1]
    head_dim = width // heads
    taps = conv_weight.shape[0]
    full_code_weight = lax.all_gather(code_weight, "dp", axis=0, tiled=True)
    joined = jnp.concatenate([inputs[0], write_proj[0], read_proj[0]], axis=1)
    rim_rows = passed_along(joined[length - (taps - 1) :], "seq", 1)
    padded = jnp.concatenate([rim_rows, joined], axis=0)
    summed = conv_bias[None, :] + conv_weight[0][None, :] * padded[0:length].astype(jnp.float32)
    for offset in range(1, taps):
        summed = summed + conv_weight[offset][None, :] * padded[offset : offset + length].astype(
            jnp.float32
        )
    active = jax.nn.silu(summed).astype(jnp.bfloat16)
    values = active[:, :width].reshape(length, heads, head_dim)
    write_all = active[:, width : width + state_dim]
    read_all = active[:, width + state_dim :]
    steps = step_size[0]
    logs = log_forget[0]
    blocks = length // SPAN
    inner_list = []
    state_list = []
    cum_list = []
    for block in range(blocks):
        lower = block * SPAN
        upper = lower + SPAN
        inner_out, states, cum_log = block_terms(
            values[lower:upper],
            write_all[lower:upper],
            read_all[lower:upper],
            steps[:, lower:upper],
            logs[:, lower:upper],
        )
        inner_list.append(inner_out)
        state_list.append(states)
        cum_list.append(cum_log)
    running = jnp.zeros((heads, head_dim, state_dim), jnp.float32)
    before = jnp.zeros((heads,), jnp.float32)
    start_list = []
    before_list = []
    for block in range(blocks):
        start_list.append(running)
        before_list.append(before)
        block_total = cum_list[block][:, -1]
        running = jnp.exp(block_total)[:, None, None] * running + state_list[block]
        before = before + block_total
    shard_logs = spread_over(before, "seq")
    carry_in, all_prior = carried_in(running, shard_logs, prior_draw)
    all_prior, carry_in = lax.optimization_barrier((all_prior, carry_in))
    outputs = []
    for block in range(blocks):
        lower = block * SPAN
        upper = lower + SPAN
        start = start_list[block] + jnp.exp(before_list[block])[:, None, None] * carry_in
        read_block = read_all[lower:upper].astype(jnp.float32)
        outer_out = jnp.exp(cum_list[block]).T[:, :, None] * jnp.einsum(
            "tn,hpn->thp", read_block, start, precision=lax.Precision.HIGHEST
        )
        outputs.append(inner_list[block] + outer_out)
    ssd_out = jnp.concatenate(outputs, axis=0)
    total = ssd_out + skip_gain[None, :, None] * values.astype(jnp.float32)
    gated = total.reshape(length, width) * jax.nn.silu(gate_proj[0].astype(jnp.float32))
    scale = lax.rsqrt(jnp.mean(gated * gated, axis=1, keepdims=True) + 1e-05)
    mixed = (gated * scale * norm_gain[None, :]).astype(jnp.bfloat16)
    pooled = jnp.mean(mixed.astype(jnp.float32).reshape(length // SEG, SEG, width), axis=1).astype(
        jnp.bfloat16
    )
    codes_local = jnp.dot(pooled, full_code_weight, preferred_element_type=jnp.float32)
    all_codes = codes_everywhere(codes_local)
    columns = jnp.concatenate([all_codes, all_prior], axis=0)
    cross = jnp.dot(codes_local, columns.T, precision=lax.Precision.HIGHEST)
    row_sq = jnp.sum(codes_local * codes_local, axis=1)
    col_sq = jnp.sum(columns * columns, axis=1)
    dist_sq = row_sq[:, None] + col_sq[None, :] - 2.0 * cross
    code_dim = codes_local.shape[1]
    kernel = 2.0 * code_dim / (2.0 * code_dim + dist_sq)
    return (mixed[None], codes_local, kernel)


def solution(mesh):
    in_specs = (
        P("dp", "seq", None),
        P("dp", "seq", None),
        P("dp", "seq", None),
        P("dp", "seq", None),
        P("dp", None, "seq"),
        P("dp", None, "seq"),
        P(),
        P(),
        P(),
        P(),
        P("dp", None),
        P(("dp", "seq"), None),
    )
    out_specs = (P("dp", "seq", None), P(("dp", "seq"), None), P(("dp", "seq"), None))
    return jax.shard_map(
        per_device, mesh=mesh, in_specs=in_specs, out_specs=out_specs, check_vma=False
    )
```

```python
import jax
import jax.numpy as jnp
from jax import lax
from jax.sharding import PartitionSpec as P

SPAN = 128
SEG = 32
CORES = 2
RING = 4
XFER = jnp.bfloat16


def passed_along(block, axis, distance):
    devices = range(lax.axis_size(axis))
    route = [(i - distance, i) for i in devices if i - distance in devices]
    return lax.ppermute(block, axis, route)


def block_terms(values, write_rows, read_rows, steps, logs):
    cum_log = jnp.cumsum(logs, axis=1)
    length = logs.shape[1]
    causal = jnp.arange(length)[:, None] >= jnp.arange(length)[None, :]
    scores = jnp.dot(read_rows, write_rows.T, preferred_element_type=jnp.float32)
    decay = jnp.exp(jnp.where(causal[None], cum_log[:, :, None] - cum_log[:, None, :], -jnp.inf))
    mixing = (scores[None] * decay * steps[:, None, :]).astype(jnp.bfloat16)
    inner_out = jnp.einsum("hts,shp->thp", mixing, values, preferred_element_type=jnp.float32)
    tail_decay = jnp.exp(cum_log[:, -1:] - cum_log) * steps
    weighted = (tail_decay[:, :, None] * write_rows.astype(jnp.float32)[None]).astype(jnp.bfloat16)
    states = jnp.einsum("hsn,shp->hpn", weighted, values, preferred_element_type=jnp.float32)
    return (inner_out, states, cum_log)


def chip_routes(seq):
    rows = seq // (CORES * RING)

    def at(x, y, c):
        return (x * RING + y) * CORES + c

    cells = [(x, y, c) for x in range(rows) for y in range(RING) for c in range(CORES)]
    partner = [(at(x, y, c), at(x, y, 1 - c)) for x, y, c in cells]
    y_fwd = [(at(x, y, c), at(x, (y + 1) % RING, c)) for x, y, c in cells]
    y_bwd = [(at(x, y, c), at(x, (y - 1) % RING, c)) for x, y, c in cells]
    x_fwd = [(at(x, y, c), at((x + 1) % rows, y, c)) for x, y, c in cells]
    x_bwd = [(at(x, y, c), at((x - 1) % rows, y, c)) for x, y, c in cells]
    return rows, partner, (y_fwd, y_bwd), (x_fwd, x_bwd)


def ring_of_four(state, fwd, bwd):
    half = state.shape[0] // 2
    sent = state.astype(XFER)
    prev_state = lax.ppermute(sent, "seq", fwd)
    next_state = lax.ppermute(sent, "seq", bwd)
    far_a = lax.ppermute(next_state[:half], "seq", bwd)
    far_b = lax.ppermute(prev_state[half:], "seq", fwd)
    far_state = jnp.concatenate([far_a, far_b], axis=0)
    return [(state, 0), (prev_state, RING - 1), (next_state, 1), (far_state, 2)]


def fold_ring(slots, pos, ring_logs):
    places = [(pos + k) % RING for (_, k) in slots]
    logs = [lax.dynamic_index_in_dim(ring_logs, p, 0, False) for p in places]
    zero = jnp.zeros_like(logs[0])
    before = None
    total = None
    for i, (value, _) in enumerate(slots):
        between = zero
        after = zero
        for j in range(len(slots)):
            if j == i:
                continue
            inside = (places[i] < places[j]) & (places[j] < pos)
            between = between + jnp.where(inside, logs[j], 0.0)
            after = after + jnp.where(places[i] < places[j], logs[j], 0.0)
        w_before = jnp.where(places[i] < pos, jnp.exp(between), 0.0)[:, None, None]
        w_total = jnp.exp(after)[:, None, None]
        v = value.astype(jnp.float32)
        before = w_before * v if before is None else before + w_before * v
        total = w_total * v if total is None else total + w_total * v
    lead = zero
    for j in range(len(slots)):
        lead = lead + jnp.where(places[j] < pos, logs[j], 0.0)
    return before, jnp.exp(lead), total


def carried_in(own_state, shard_logs):
    seq = lax.axis_size("seq")
    rows, partner, y_routes, x_routes = chip_routes(seq)
    assert rows == RING and seq == rows * RING * CORES
    place = lax.axis_index("seq")
    core = place % CORES
    y_pos = (place // CORES) % RING
    x_pos = place // (CORES * RING)
    half = own_state.shape[0] // CORES
    mine = core * half
    theirs = (1 - core) * half
    grid_logs = shard_logs.reshape(rows, RING, CORES, -1)
    chip_logs = lax.dynamic_slice_in_dim(grid_logs[:, :, 0] + grid_logs[:, :, 1], mine, half, 2)
    low_log = lax.dynamic_slice_in_dim(grid_logs[x_pos, y_pos, 0], mine, half, 0)
    high_log = lax.dynamic_slice_in_dim(grid_logs[x_pos, y_pos, 1], mine, half, 0)
    own_half = lax.dynamic_slice_in_dim(own_state, mine, half, 0)
    other_half = lax.ppermute(lax.dynamic_slice_in_dim(own_state, theirs, half, 0), "seq", partner)
    low_half = jnp.where(core == 0, own_half, other_half)
    high_half = jnp.where(core == 0, other_half, own_half)
    chip_state = jnp.exp(high_log)[:, None, None] * low_half + high_half
    slots = ring_of_four(chip_state, *y_routes)
    row_logs = lax.dynamic_index_in_dim(chip_logs, x_pos, 0, False)
    row_before, row_lead, row_total = fold_ring(slots, y_pos, row_logs)
    slots = ring_of_four(row_total, *x_routes)
    rows_before, _, _ = fold_ring(slots, x_pos, jnp.sum(chip_logs, axis=1))
    chip_in = row_lead[:, None, None] * rows_before + row_before
    high_in = jnp.exp(low_log)[:, None, None] * chip_in + low_half
    keep = jnp.where(core == 0, chip_in, high_in)
    give = jnp.where(core == 0, high_in, chip_in)
    got = lax.ppermute(give, "seq", partner)
    return jnp.where(core == 0, jnp.concatenate([keep, got], 0), jnp.concatenate([got, keep], 0))


def placed(block, slots, index):
    held = jnp.zeros((slots,) + block.shape, block.dtype)
    return lax.dynamic_update_index_in_dim(held, block, index, 0)


def spread_over(block, axis):
    count = lax.axis_size(axis)
    return lax.all_to_all(jnp.broadcast_to(block[None], (count,) + block.shape), axis, 0, 0)


def prior_everywhere(block):
    rows = spread_over(block, "seq").reshape((-1,) + block.shape[1:])
    return lax.all_gather(rows, "dp", axis=0, tiled=True)


def rows_everywhere(block):
    rows = spread_over(block.astype(XFER), "dp")
    got = spread_over(rows, "seq")
    return jnp.swapaxes(got, 0, 1).astype(jnp.float32)


def per_device(
    inputs,
    gate_proj,
    write_proj,
    read_proj,
    step_size,
    log_forget,
    conv_weight,
    conv_bias,
    skip_gain,
    norm_gain,
    code_weight,
    prior_draw,
):
    length = inputs.shape[1]
    width = inputs.shape[2]
    state_dim = write_proj.shape[2]
    heads = step_size.shape[1]
    head_dim = width // heads
    taps = conv_weight.shape[0]
    full_code_weight = lax.all_gather(code_weight, "dp", axis=0, tiled=True)
    joined = jnp.concatenate([inputs[0], write_proj[0], read_proj[0]], axis=1)
    rim_rows = passed_along(joined[length - (taps - 1) :], "seq", 1)
    padded = jnp.concatenate([rim_rows, joined], axis=0)
    summed = conv_bias[None, :] + conv_weight[0][None, :] * padded[0:length].astype(jnp.float32)
    for offset in range(1, taps):
        summed = summed + conv_weight[offset][None, :] * padded[offset : offset + length].astype(
            jnp.float32
        )
    active = jax.nn.silu(summed).astype(jnp.bfloat16)
    values = active[:, :width].reshape(length, heads, head_dim)
    write_all = active[:, width : width + state_dim]
    read_all = active[:, width + state_dim :]
    steps = step_size[0]
    logs = log_forget[0]
    blocks = length // SPAN
    inner_list = []
    state_list = []
    cum_list = []
    for block in range(blocks):
        lower = block * SPAN
        upper = lower + SPAN
        inner_out, states, cum_log = block_terms(
            values[lower:upper],
            write_all[lower:upper],
            read_all[lower:upper],
            steps[:, lower:upper],
            logs[:, lower:upper],
        )
        inner_list.append(inner_out)
        state_list.append(states)
        cum_list.append(cum_log)
    running = jnp.zeros((heads, head_dim, state_dim), jnp.float32)
    before = jnp.zeros((heads,), jnp.float32)
    start_list = []
    before_list = []
    for block in range(blocks):
        start_list.append(running)
        before_list.append(before)
        block_total = cum_list[block][:, -1]
        running = jnp.exp(block_total)[:, None, None] * running + state_list[block]
        before = before + block_total
    shard_logs = spread_over(before, "seq")
    carry_in = carried_in(running, shard_logs)
    outputs = []
    for block in range(blocks):
        lower = block * SPAN
        upper = lower + SPAN
        start = start_list[block] + jnp.exp(before_list[block])[:, None, None] * carry_in
        read_block = read_all[lower:upper].astype(jnp.float32)
        outer_out = jnp.exp(cum_list[block]).T[:, :, None] * jnp.einsum(
            "tn,hpn->thp", read_block, start, precision=lax.Precision.HIGHEST
        )
        outputs.append(inner_list[block] + outer_out)
    ssd_out = jnp.concatenate(outputs, axis=0)
    total = ssd_out + skip_gain[None, :, None] * values.astype(jnp.float32)
    gated = total.reshape(length, width) * jax.nn.silu(gate_proj[0].astype(jnp.float32))
    scale = lax.rsqrt(jnp.mean(gated * gated, axis=1, keepdims=True) + 1e-05)
    mixed = (gated * scale * norm_gain[None, :]).astype(jnp.bfloat16)
    pooled = jnp.mean(mixed.astype(jnp.float32).reshape(length // SEG, SEG, width), axis=1).astype(
        jnp.bfloat16
    )
    codes_local = jnp.dot(pooled, full_code_weight, preferred_element_type=jnp.float32)
    local_rows = codes_local.shape[0]
    code_dim = codes_local.shape[1]
    both = rows_everywhere(jnp.concatenate([codes_local, prior_draw], axis=0))
    all_codes = both[:, :, :local_rows].reshape(-1, code_dim)
    all_prior = both[:, :, local_rows:].reshape(-1, code_dim)
    columns = jnp.concatenate([all_codes, all_prior], axis=0)
    cross = jnp.dot(codes_local, columns.T, precision=lax.Precision.HIGHEST)
    row_sq = jnp.sum(codes_local * codes_local, axis=1)
    col_sq = jnp.sum(columns * columns, axis=1)
    dist_sq = row_sq[:, None] + col_sq[None, :] - 2.0 * cross
    code_dim = codes_local.shape[1]
    kernel = 2.0 * code_dim / (2.0 * code_dim + dist_sq)
    return (mixed[None], codes_local, kernel)


def solution(mesh):
    in_specs = (
        P("dp", "seq", None),
        P("dp", "seq", None),
        P("dp", "seq", None),
        P("dp", "seq", None),
        P("dp", None, "seq"),
        P("dp", None, "seq"),
        P(),
        P(),
        P(),
        P(),
        P("dp", None),
        P(("dp", "seq"), None),
    )
    out_specs = (P("dp", "seq", None), P(("dp", "seq"), None), P(("dp", "seq"), None))
    return jax.shard_map(
        per_device, mesh=mesh, in_specs=in_specs, out_specs=out_specs, check_vma=False
    )
```

```python
import jax
import jax.numpy as jnp
from jax import lax
from jax.sharding import PartitionSpec as P

SPAN = 128
SEG = 32
CORES = 2
RING = 4
XFER = jnp.bfloat16


def passed_along(block, axis, distance):
    devices = range(lax.axis_size(axis))
    route = [(i - distance, i) for i in devices if i - distance in devices]
    return lax.ppermute(block, axis, route)


def block_terms(values, write_rows, read_rows, steps, logs):
    cum_log = jnp.cumsum(logs, axis=1)
    length = logs.shape[1]
    causal = jnp.arange(length)[:, None] >= jnp.arange(length)[None, :]
    scores = jnp.dot(read_rows, write_rows.T, preferred_element_type=jnp.float32)
    decay = jnp.exp(jnp.where(causal[None], cum_log[:, :, None] - cum_log[:, None, :], -jnp.inf))
    mixing = (scores[None] * decay * steps[:, None, :]).astype(jnp.bfloat16)
    inner_out = jnp.einsum("hts,shp->thp", mixing, values, preferred_element_type=jnp.float32)
    tail_decay = jnp.exp(cum_log[:, -1:] - cum_log) * steps
    weighted = (tail_decay[:, :, None] * write_rows.astype(jnp.float32)[None]).astype(jnp.bfloat16)
    states = jnp.einsum("hsn,shp->hpn", weighted, values, preferred_element_type=jnp.float32)
    return (inner_out, states, cum_log)


def chip_routes(seq):
    rows = seq // (CORES * RING)

    def at(x, y, c):
        return (x * RING + y) * CORES + c

    cells = [(x, y, c) for x in range(rows) for y in range(RING) for c in range(CORES)]
    partner = [(at(x, y, c), at(x, y, 1 - c)) for x, y, c in cells]
    y_fwd = [(at(x, y, c), at(x, (y + 1) % RING, c)) for x, y, c in cells]
    y_bwd = [(at(x, y, c), at(x, (y - 1) % RING, c)) for x, y, c in cells]
    x_fwd = [(at(x, y, c), at((x + 1) % rows, y, c)) for x, y, c in cells]
    x_bwd = [(at(x, y, c), at((x - 1) % rows, y, c)) for x, y, c in cells]
    return rows, partner, (y_fwd, y_bwd), (x_fwd, x_bwd)


def ring_of_four(state, fwd, bwd):
    half = state.shape[0] // 2
    sent = state.astype(XFER)
    prev_state = lax.ppermute(sent, "seq", fwd)
    next_state = lax.ppermute(sent, "seq", bwd)
    far_a = lax.ppermute(next_state[:half], "seq", bwd)
    far_b = lax.ppermute(prev_state[half:], "seq", fwd)
    far_state = jnp.concatenate([far_a, far_b], axis=0)
    return [(state, 0), (prev_state, RING - 1), (next_state, 1), (far_state, 2)]


def fold_ring(slots, pos, ring_logs):
    places = [(pos + k) % RING for (_, k) in slots]
    logs = [lax.dynamic_index_in_dim(ring_logs, p, 0, False) for p in places]
    zero = jnp.zeros_like(logs[0])
    before = None
    total = None
    for i, (value, _) in enumerate(slots):
        between = zero
        after = zero
        for j in range(len(slots)):
            if j == i:
                continue
            inside = (places[i] < places[j]) & (places[j] < pos)
            between = between + jnp.where(inside, logs[j], 0.0)
            after = after + jnp.where(places[i] < places[j], logs[j], 0.0)
        w_before = jnp.where(places[i] < pos, jnp.exp(between), 0.0)[:, None, None]
        w_total = jnp.exp(after)[:, None, None]
        v = value.astype(jnp.float32)
        before = w_before * v if before is None else before + w_before * v
        total = w_total * v if total is None else total + w_total * v
    lead = zero
    for j in range(len(slots)):
        lead = lead + jnp.where(places[j] < pos, logs[j], 0.0)
    return before, jnp.exp(lead), total


def carried_in(own_state, shard_logs):
    seq = lax.axis_size("seq")
    rows, partner, y_routes, x_routes = chip_routes(seq)
    assert rows == RING and seq == rows * RING * CORES
    place = lax.axis_index("seq")
    core = place % CORES
    y_pos = (place // CORES) % RING
    x_pos = place // (CORES * RING)
    half = own_state.shape[0] // CORES
    mine = core * half
    theirs = (1 - core) * half
    grid_logs = shard_logs.reshape(rows, RING, CORES, -1)
    chip_logs = lax.dynamic_slice_in_dim(grid_logs[:, :, 0] + grid_logs[:, :, 1], mine, half, 2)
    low_log = lax.dynamic_slice_in_dim(grid_logs[x_pos, y_pos, 0], mine, half, 0)
    high_log = lax.dynamic_slice_in_dim(grid_logs[x_pos, y_pos, 1], mine, half, 0)
    own_half = lax.dynamic_slice_in_dim(own_state, mine, half, 0)
    other_half = lax.ppermute(lax.dynamic_slice_in_dim(own_state, theirs, half, 0), "seq", partner)
    low_half = jnp.where(core == 0, own_half, other_half)
    high_half = jnp.where(core == 0, other_half, own_half)
    chip_state = jnp.exp(high_log)[:, None, None] * low_half + high_half
    slots = ring_of_four(chip_state, *y_routes)
    row_logs = lax.dynamic_index_in_dim(chip_logs, x_pos, 0, False)
    row_before, row_lead, row_total = fold_ring(slots, y_pos, row_logs)
    slots = ring_of_four(row_total, *x_routes)
    rows_before, _, _ = fold_ring(slots, x_pos, jnp.sum(chip_logs, axis=1))
    chip_in = row_lead[:, None, None] * rows_before + row_before
    high_in = jnp.exp(low_log)[:, None, None] * chip_in + low_half
    keep = jnp.where(core == 0, chip_in, high_in)
    give = jnp.where(core == 0, high_in, chip_in)
    got = lax.ppermute(give, "seq", partner)
    return jnp.where(core == 0, jnp.concatenate([keep, got], 0), jnp.concatenate([got, keep], 0))


def placed(block, slots, index):
    held = jnp.zeros((slots,) + block.shape, block.dtype)
    return lax.dynamic_update_index_in_dim(held, block, index, 0)


def spread_over(block, axis):
    count = lax.axis_size(axis)
    return lax.all_to_all(jnp.broadcast_to(block[None], (count,) + block.shape), axis, 0, 0)


def prior_everywhere(block):
    rows = spread_over(block, "seq").reshape((-1,) + block.shape[1:])
    return lax.all_gather(rows, "dp", axis=0, tiled=True)


def rows_everywhere(block):
    rows = spread_over(block.astype(XFER), "dp")
    got = spread_over(rows, "seq")
    return jnp.swapaxes(got, 0, 1).astype(jnp.float32)


def per_device(
    inputs,
    gate_proj,
    write_proj,
    read_proj,
    step_size,
    log_forget,
    conv_weight,
    conv_bias,
    skip_gain,
    norm_gain,
    code_weight,
    prior_draw,
):
    length = inputs.shape[1]
    width = inputs.shape[2]
    state_dim = write_proj.shape[2]
    heads = step_size.shape[1]
    head_dim = width // heads
    taps = conv_weight.shape[0]
    full_code_weight = lax.all_gather(code_weight, "dp", axis=0, tiled=True)
    joined = jnp.concatenate([inputs[0], write_proj[0], read_proj[0]], axis=1)
    rim_rows = passed_along(joined[length - (taps - 1) :], "seq", 1)
    padded = jnp.concatenate([rim_rows, joined], axis=0)
    summed = conv_bias[None, :] + conv_weight[0][None, :] * padded[0:length].astype(jnp.float32)
    for offset in range(1, taps):
        summed = summed + conv_weight[offset][None, :] * padded[offset : offset + length].astype(
            jnp.float32
        )
    active = jax.nn.silu(summed).astype(jnp.bfloat16)
    shard_total = jnp.zeros((heads,), jnp.float32)
    for block in range(length // SPAN):
        shard_total = shard_total + jnp.cumsum(log_forget[0][:, block * SPAN : (block + 1) * SPAN], axis=1)[:, -1]
    active, shard_logs = lax.optimization_barrier((active, spread_over(shard_total, "seq")))
    values = active[:, :width].reshape(length, heads, head_dim)
    write_all = active[:, width : width + state_dim]
    read_all = active[:, width + state_dim :]
    steps = step_size[0]
    logs = log_forget[0]
    blocks = length // SPAN
    inner_list = []
    state_list = []
    cum_list = []
    for block in range(blocks):
        lower = block * SPAN
        upper = lower + SPAN
        inner_out, states, cum_log = block_terms(
            values[lower:upper],
            write_all[lower:upper],
            read_all[lower:upper],
            steps[:, lower:upper],
            logs[:, lower:upper],
        )
        inner_list.append(inner_out)
        state_list.append(states)
        cum_list.append(cum_log)
    running = jnp.zeros((heads, head_dim, state_dim), jnp.float32)
    before = jnp.zeros((heads,), jnp.float32)
    start_list = []
    before_list = []
    for block in range(blocks):
        start_list.append(running)
        before_list.append(before)
        block_total = cum_list[block][:, -1]
        running = jnp.exp(block_total)[:, None, None] * running + state_list[block]
        before = before + block_total
    carry_in = carried_in(running, shard_logs)
    outputs = []
    for block in range(blocks):
        lower = block * SPAN
        upper = lower + SPAN
        start = start_list[block] + jnp.exp(before_list[block])[:, None, None] * carry_in
        read_block = read_all[lower:upper].astype(jnp.float32)
        outer_out = jnp.exp(cum_list[block]).T[:, :, None] * jnp.einsum(
            "tn,hpn->thp", read_block, start, precision=lax.Precision.HIGHEST
        )
        outputs.append(inner_list[block] + outer_out)
    ssd_out = jnp.concatenate(outputs, axis=0)
    total = ssd_out + skip_gain[None, :, None] * values.astype(jnp.float32)
    gated = total.reshape(length, width) * jax.nn.silu(gate_proj[0].astype(jnp.float32))
    scale = lax.rsqrt(jnp.mean(gated * gated, axis=1, keepdims=True) + 1e-05)
    mixed = (gated * scale * norm_gain[None, :]).astype(jnp.bfloat16)
    pooled = jnp.mean(mixed.astype(jnp.float32).reshape(length // SEG, SEG, width), axis=1).astype(
        jnp.bfloat16
    )
    codes_local = jnp.dot(pooled, full_code_weight, preferred_element_type=jnp.float32)
    local_rows = codes_local.shape[0]
    code_dim = codes_local.shape[1]
    both = rows_everywhere(jnp.concatenate([codes_local, prior_draw], axis=0))
    all_codes = both[:, :, :local_rows].reshape(-1, code_dim)
    all_prior = both[:, :, local_rows:].reshape(-1, code_dim)
    columns = jnp.concatenate([all_codes, all_prior], axis=0)
    cross = jnp.dot(codes_local, columns.T, precision=lax.Precision.HIGHEST)
    row_sq = jnp.sum(codes_local * codes_local, axis=1)
    col_sq = jnp.sum(columns * columns, axis=1)
    dist_sq = row_sq[:, None] + col_sq[None, :] - 2.0 * cross
    code_dim = codes_local.shape[1]
    kernel = 2.0 * code_dim / (2.0 * code_dim + dist_sq)
    return (mixed[None], codes_local, kernel)


def solution(mesh):
    in_specs = (
        P("dp", "seq", None),
        P("dp", "seq", None),
        P("dp", "seq", None),
        P("dp", "seq", None),
        P("dp", None, "seq"),
        P("dp", None, "seq"),
        P(),
        P(),
        P(),
        P(),
        P("dp", None),
        P(("dp", "seq"), None),
    )
    out_specs = (P("dp", "seq", None), P(("dp", "seq"), None), P(("dp", "seq"), None))
    return jax.shard_map(
        per_device, mesh=mesh, in_specs=in_specs, out_specs=out_specs, check_vma=False
    )
```

```python
import jax
import jax.numpy as jnp
from jax import lax
from jax.sharding import PartitionSpec as P

SPAN = 128
SEG = 32
CORES = 2
RING = 4
XFER = jnp.bfloat16


def passed_along(block, axis, distance):
    devices = range(lax.axis_size(axis))
    route = [(i - distance, i) for i in devices if i - distance in devices]
    return lax.ppermute(block, axis, route)


def block_terms(values, write_rows, read_rows, steps, logs):
    cum_log = jnp.cumsum(logs, axis=1)
    length = logs.shape[1]
    causal = jnp.arange(length)[:, None] >= jnp.arange(length)[None, :]
    scores = jnp.dot(read_rows, write_rows.T, preferred_element_type=jnp.float32)
    decay = jnp.exp(jnp.where(causal[None], cum_log[:, :, None] - cum_log[:, None, :], -jnp.inf))
    mixing = (scores[None] * decay * steps[:, None, :]).astype(jnp.bfloat16)
    inner_out = jnp.einsum("hts,shp->thp", mixing, values, preferred_element_type=jnp.float32)
    tail_decay = jnp.exp(cum_log[:, -1:] - cum_log) * steps
    weighted = (tail_decay[:, :, None] * write_rows.astype(jnp.float32)[None]).astype(jnp.bfloat16)
    states = jnp.einsum("hsn,shp->hpn", weighted, values, preferred_element_type=jnp.float32)
    return (inner_out, states, cum_log)


def chip_routes(seq):
    rows = seq // (CORES * RING)

    def at(x, y, c):
        return (x * RING + y) * CORES + c

    cells = [(x, y, c) for x in range(rows) for y in range(RING) for c in range(CORES)]
    partner = [(at(x, y, c), at(x, y, 1 - c)) for x, y, c in cells]
    y_fwd = [(at(x, y, c), at(x, (y + 1) % RING, c)) for x, y, c in cells]
    y_bwd = [(at(x, y, c), at(x, (y - 1) % RING, c)) for x, y, c in cells]
    x_fwd = [(at(x, y, c), at((x + 1) % rows, y, c)) for x, y, c in cells]
    x_bwd = [(at(x, y, c), at((x - 1) % rows, y, c)) for x, y, c in cells]
    return rows, partner, (y_fwd, y_bwd), (x_fwd, x_bwd)


def ring_of_four(state, fwd, bwd):
    half = state.shape[0] // 2
    sent = state.astype(XFER)
    prev_state = lax.ppermute(sent, "seq", fwd)
    next_state = lax.ppermute(sent, "seq", bwd)
    far_a = lax.ppermute(next_state[:half], "seq", bwd)
    far_b = lax.ppermute(prev_state[half:], "seq", fwd)
    far_state = jnp.concatenate([far_a, far_b], axis=0)
    return [(state, 0), (prev_state, RING - 1), (next_state, 1), (far_state, 2)]


def fold_ring(slots, pos, ring_logs):
    places = [(pos + k) % RING for (_, k) in slots]
    logs = [lax.dynamic_index_in_dim(ring_logs, p, 0, False) for p in places]
    zero = jnp.zeros_like(logs[0])
    before = None
    total = None
    for i, (value, _) in enumerate(slots):
        between = zero
        after = zero
        for j in range(len(slots)):
            if j == i:
                continue
            inside = (places[i] < places[j]) & (places[j] < pos)
            between = between + jnp.where(inside, logs[j], 0.0)
            after = after + jnp.where(places[i] < places[j], logs[j], 0.0)
        w_before = jnp.where(places[i] < pos, jnp.exp(between), 0.0)[:, None, None]
        w_total = jnp.exp(after)[:, None, None]
        v = value.astype(jnp.float32)
        before = w_before * v if before is None else before + w_before * v
        total = w_total * v if total is None else total + w_total * v
    lead = zero
    for j in range(len(slots)):
        lead = lead + jnp.where(places[j] < pos, logs[j], 0.0)
    return before, jnp.exp(lead), total


def carried_in(own_state, shard_logs):
    seq = lax.axis_size("seq")
    rows, partner, y_routes, x_routes = chip_routes(seq)
    assert rows == RING and seq == rows * RING * CORES
    place = lax.axis_index("seq")
    core = place % CORES
    y_pos = (place // CORES) % RING
    x_pos = place // (CORES * RING)
    half = own_state.shape[0] // CORES
    mine = core * half
    theirs = (1 - core) * half
    grid_logs = shard_logs.reshape(rows, RING, CORES, -1)
    chip_logs = lax.dynamic_slice_in_dim(grid_logs[:, :, 0] + grid_logs[:, :, 1], mine, half, 2)
    low_log = lax.dynamic_slice_in_dim(grid_logs[x_pos, y_pos, 0], mine, half, 0)
    high_log = lax.dynamic_slice_in_dim(grid_logs[x_pos, y_pos, 1], mine, half, 0)
    own_half = lax.dynamic_slice_in_dim(own_state, mine, half, 0)
    other_half = lax.ppermute(lax.dynamic_slice_in_dim(own_state, theirs, half, 0), "seq", partner)
    low_half = jnp.where(core == 0, own_half, other_half)
    high_half = jnp.where(core == 0, other_half, own_half)
    chip_state = jnp.exp(high_log)[:, None, None] * low_half + high_half
    slots = ring_of_four(chip_state, *y_routes)
    row_logs = lax.dynamic_index_in_dim(chip_logs, x_pos, 0, False)
    row_before, row_lead, row_total = fold_ring(slots, y_pos, row_logs)
    slots = ring_of_four(row_total, *x_routes)
    rows_before, _, _ = fold_ring(slots, x_pos, jnp.sum(chip_logs, axis=1))
    chip_in = row_lead[:, None, None] * rows_before + row_before
    high_in = jnp.exp(low_log)[:, None, None] * chip_in + low_half
    keep = jnp.where(core == 0, chip_in, high_in)
    give = jnp.where(core == 0, high_in, chip_in)
    got = lax.ppermute(give, "seq", partner)
    return jnp.where(core == 0, jnp.concatenate([keep, got], 0), jnp.concatenate([got, keep], 0))


def placed(block, slots, index):
    held = jnp.zeros((slots,) + block.shape, block.dtype)
    return lax.dynamic_update_index_in_dim(held, block, index, 0)


def spread_over(block, axis):
    count = lax.axis_size(axis)
    return lax.all_to_all(jnp.broadcast_to(block[None], (count,) + block.shape), axis, 0, 0)


def prior_everywhere(block):
    rows = spread_over(block, "seq").reshape((-1,) + block.shape[1:])
    return lax.all_gather(rows, "dp", axis=0, tiled=True)


def rows_everywhere(block):
    rows = spread_over(block.astype(XFER), "dp")
    got = spread_over(rows, "seq")
    return jnp.swapaxes(got, 0, 1).astype(jnp.float32)


def per_device(
    inputs,
    gate_proj,
    write_proj,
    read_proj,
    step_size,
    log_forget,
    conv_weight,
    conv_bias,
    skip_gain,
    norm_gain,
    code_weight,
    prior_draw,
):
    length = inputs.shape[1]
    width = inputs.shape[2]
    state_dim = write_proj.shape[2]
    heads = step_size.shape[1]
    head_dim = width // heads
    taps = conv_weight.shape[0]
    full_code_weight = lax.all_gather(code_weight, "dp", axis=0, tiled=True)
    joined = jnp.concatenate([inputs[0], write_proj[0], read_proj[0]], axis=1)
    rim_rows = passed_along(joined[length - (taps - 1) :], "seq", 1)
    padded = jnp.concatenate([rim_rows, joined], axis=0)
    summed = conv_bias[None, :] + conv_weight[0][None, :] * padded[0:length].astype(jnp.float32)
    for offset in range(1, taps):
        summed = summed + conv_weight[offset][None, :] * padded[offset : offset + length].astype(
            jnp.float32
        )
    active = jax.nn.silu(summed).astype(jnp.bfloat16)
    shard_total = jnp.zeros((heads,), jnp.float32)
    for block in range(length // SPAN):
        shard_total = shard_total + jnp.cumsum(log_forget[0][:, block * SPAN : (block + 1) * SPAN], axis=1)[:, -1]
    active, shard_logs = lax.optimization_barrier((active, spread_over(shard_total, "seq")))
    values = active[:, :width].reshape(length, heads, head_dim)
    write_all = active[:, width : width + state_dim]
    read_all = active[:, width + state_dim :]
    steps = step_size[0]
    logs = log_forget[0]
    blocks = length // SPAN
    inner_list = []
    state_list = []
    cum_list = []
    for block in range(blocks):
        lower = block * SPAN
        upper = lower + SPAN
        inner_out, states, cum_log = block_terms(
            values[lower:upper],
            write_all[lower:upper],
            read_all[lower:upper],
            steps[:, lower:upper],
            logs[:, lower:upper],
        )
        inner_list.append(inner_out)
        state_list.append(states)
        cum_list.append(cum_log)
    running = jnp.zeros((heads, head_dim, state_dim), jnp.float32)
    before = jnp.zeros((heads,), jnp.float32)
    start_list = []
    before_list = []
    for block in range(blocks):
        start_list.append(running)
        before_list.append(before)
        block_total = cum_list[block][:, -1]
        running = jnp.exp(block_total)[:, None, None] * running + state_list[block]
        before = before + block_total
    carry_in = carried_in(running, shard_logs)
    outputs = []
    for block in range(blocks):
        lower = block * SPAN
        upper = lower + SPAN
        start = start_list[block] + jnp.exp(before_list[block])[:, None, None] * carry_in
        read_block = read_all[lower:upper]
        start_hi = lax.reduce_precision(start, exponent_bits=8, mantissa_bits=7)
        start_lo = start - start_hi
        pieces = [jnp.einsum("tn,hpn->thp", read_block, piece.astype(jnp.bfloat16), preferred_element_type=jnp.float32) for piece in (start_hi, start_lo)]
        outer_out = jnp.exp(cum_list[block]).T[:, :, None] * (pieces[0] + pieces[1])
        outputs.append(inner_list[block] + outer_out)
    ssd_out = jnp.concatenate(outputs, axis=0)
    total = ssd_out + skip_gain[None, :, None] * values.astype(jnp.float32)
    gated = total.reshape(length, width) * jax.nn.silu(gate_proj[0].astype(jnp.float32))
    scale = lax.rsqrt(jnp.mean(gated * gated, axis=1, keepdims=True) + 1e-05)
    mixed = (gated * scale * norm_gain[None, :]).astype(jnp.bfloat16)
    pooled = jnp.mean(mixed.astype(jnp.float32).reshape(length // SEG, SEG, width), axis=1).astype(
        jnp.bfloat16
    )
    codes_local = jnp.dot(pooled, full_code_weight, preferred_element_type=jnp.float32)
    local_rows = codes_local.shape[0]
    code_dim = codes_local.shape[1]
    both = rows_everywhere(jnp.concatenate([codes_local, prior_draw], axis=0))
    all_codes = both[:, :, :local_rows].reshape(-1, code_dim)
    all_prior = both[:, :, local_rows:].reshape(-1, code_dim)
    columns = jnp.concatenate([all_codes, all_prior], axis=0)
    cross = jnp.dot(codes_local, columns.T, precision=lax.Precision.HIGHEST)
    row_sq = jnp.sum(codes_local * codes_local, axis=1)
    col_sq = jnp.sum(columns * columns, axis=1)
    dist_sq = row_sq[:, None] + col_sq[None, :] - 2.0 * cross
    code_dim = codes_local.shape[1]
    kernel = 2.0 * code_dim / (2.0 * code_dim + dist_sq)
    return (mixed[None], codes_local, kernel)


def solution(mesh):
    in_specs = (
        P("dp", "seq", None),
        P("dp", "seq", None),
        P("dp", "seq", None),
        P("dp", "seq", None),
        P("dp", None, "seq"),
        P("dp", None, "seq"),
        P(),
        P(),
        P(),
        P(),
        P("dp", None),
        P(("dp", "seq"), None),
    )
    out_specs = (P("dp", "seq", None), P(("dp", "seq"), None), P(("dp", "seq"), None))
    return jax.shard_map(
        per_device, mesh=mesh, in_specs=in_specs, out_specs=out_specs, check_vma=False
    )
```
